32 devices in a mesh: row: 4 (over z), col: 8 (over y, x, core).
Axes of the slice: x: 2, y: 2, z: 4, core: 2. Of those that a mesh axis runs over, the one named last changes fastest.
Arguments:
- factor_rows: float32 [2, 1024, 4096], P(None, 'col', 'row'), as said below
- adjoint_rows: float32 [2, 1024, 4096], P(None, 'col', 'row'), as said below
- panel_inverse: float32 [2, 1024, 1024], replicated, as said below
Outputs:
- kernel_adjoint: float32 [2, 1024, 4096], P(None, 'col', 'row')
Inputs may be any that keep to these rules, and one draw needn't show every extreme that they name: `factor_rows`: zero right of the diagonal; in panel p the columns J_p hold a lower-triangular block with diagonal entries from 0.5 to 4. `adjoint_rows`: zero right of the diagonal of the same rows. panel_inverse[p] is the inverse of factor_rows[p, :, J_p] to float32 rounding.
All inputs are finite; a program needn't handle non-finite values.
Results may differ from the reference program's by a relative error of at most 0.0001.
Values sent between devices are 32-bit elements; how exact they have to be, the bound alone decides.
No kernel may reach another device: no remote copies, remote signals or barrier semaphores. Data moves between devices by JAX's collectives and lax.ppermute only.
A program may use at most 128 MiB of HBM per device.

```python
import math
import jax
import jax.numpy as jnp
from jax import lax

B = 1024
PAN = 2
M = 4096


def diag_blocks(key):
    base_key = jax.random.fold_in(key, 17)
    key_diag, key_low = jax.random.split(base_key)
    diag_vals = jax.random.uniform(key_diag, (PAN, B), jnp.float32, 1.0, 2.0)
    strict = jax.random.normal(key_low, (PAN, B, B), jnp.float32) * (0.3 / math.sqrt(B))
    unit_diag = jnp.eye(B, dtype=jnp.float32)
    return jnp.tril(strict, -1) + diag_vals[:, :, None] * unit_diag


def draw_panel_inverse(key, part):
    blocks = diag_blocks(key)
    unit_diag = jnp.eye(B, dtype=jnp.float32)
    return jax.vmap(lambda block: jax.scipy.linalg.solve_triangular(block, unit_diag, lower=True))(blocks)


def draw_factor_rows(key, part):
    blocks = diag_blocks(key)
    first_col = M - PAN * B
    sub_key = jax.random.fold_in(key, 29)
    left_vals = jax.random.normal(sub_key, (PAN, B, M), jnp.float32) / math.sqrt(B)
    pieces = []
    for panel in range(PAN):
        low_col = first_col + panel * B
        row_block = jnp.concatenate([left_vals[panel, :, :low_col], blocks[panel], jnp.zeros((B, M - low_col - B), jnp.float32)], axis=1)
        pieces.append(row_block)
    return jnp.stack(pieces)


def draw_adjoint_rows(key, part):
    first_col = M - PAN * B
    sub_key = jax.random.fold_in(key, 43)
    values = jax.random.normal(sub_key, (PAN, B, M), jnp.float32)
    global_row = first_col + jnp.arange(PAN, dtype=jnp.int32)[:, None, None] * B + jnp.arange(B, dtype=jnp.int32)[None, :, None]
    columns = jnp.arange(M, dtype=jnp.int32)[None, None, :]
    return jnp.where(columns <= global_row, values, 0.0)


def setup_inputs(seed: int = 0) -> dict:
    splits = jax.random.split(jax.random.key(seed), 4)
    return {
        "factor_rows": draw_factor_rows(jax.random.fold_in(splits[3], 71), 0),
        "adjoint_rows": draw_adjoint_rows(jax.random.fold_in(splits[3], 71), 0),
        "panel_inverse": draw_panel_inverse(jax.random.fold_in(splits[3], 71), 0),
    }


HIGHEST = lax.Precision.HIGHEST

def phi_lower(matrix):
    unit_diag = jnp.eye(matrix.shape[0], dtype=jnp.float32)
    return jnp.tril(matrix) * (1.0 - 0.5 * unit_diag)

def product(left_mat, right_mat):
    return jnp.dot(left_mat.astype(jnp.float32), right_mat.astype(jnp.float32), precision=HIGHEST, preferred_element_type=jnp.float32)

def diag_fix(factor, diag_pre, inverse):
    inner = phi_lower(product(factor.T, diag_pre))
    return phi_lower(product(product(inverse.T, inner + inner.T), inverse))

def reference(factor_rows, adjoint_rows, panel_inverse):
    first_col = M - PAN * B
    adjoint = adjoint_rows
    for panel in range(PAN - 1, -1, -1):
        low_col = first_col + panel * B
        high_col = low_col + B
        inverse = panel_inverse[panel]
        col_adjoint = jnp.einsum('qib,bj->qij', adjoint[panel + 1:, :, low_col:high_col], inverse, precision=HIGHEST)
        below_block = factor_rows[panel + 1:, :, low_col:high_col]
        diag_pre = jnp.tril(adjoint[panel, :, low_col:high_col] - jnp.einsum('qbi,qbj->ij', col_adjoint, below_block, precision=HIGHEST))
        diag_new = diag_fix(factor_rows[panel, :, low_col:high_col], diag_pre, inverse)
        row_panel = factor_rows[panel, :, :low_col]
        left_block = factor_rows[panel + 1:, :, :low_col]
        block_update = jnp.einsum('qib,bj->qij', col_adjoint, row_panel, precision=HIGHEST)
        cross_term = jnp.einsum('qbi,qbj->ij', col_adjoint, left_block, precision=HIGHEST)
        row_update = cross_term + product(diag_new + diag_new.T, row_panel)
        adjoint = adjoint.at[panel + 1:, :, :low_col].add(-block_update)
        adjoint = adjoint.at[panel, :, :low_col].add(-row_update)
        adjoint = adjoint.at[panel + 1:, :, low_col:high_col].set(col_adjoint)
        adjoint = adjoint.at[panel, :, low_col:high_col].set(diag_new)
    return adjoint
```

```python
import jax
import jax.numpy as jnp
from jax import lax
from jax.sharding import PartitionSpec as P

HIGHEST = lax.Precision.HIGHEST


def mm(left, right):
    return jnp.dot(left, right, precision=HIGHEST, preferred_element_type=jnp.float32)


def tmm(left, right):
    return lax.dot_general(left, right, (((0,), (0,)), ((), ())), precision=HIGHEST,
                           preferred_element_type=jnp.float32)


def phi_sym(matrix):
    eye = jnp.eye(matrix.shape[0], dtype=jnp.float32)
    half = jnp.tril(matrix) * (1.0 - 0.5 * eye)
    return half + half.T


def row_bcast(value, source, targets):
    row = lax.axis_index("row")
    recv = None
    for target in targets:
        got = lax.ppermute(value, "row", [(source, target)])
        recv = got if recv is None else recv + got
    if recv is None:
        return value
    return jnp.where(row == source, value, recv)


def local(factor_rows, adjoint_rows, panel_inverse):
    row_count = lax.axis_size("row")
    panels = panel_inverse.shape[0]
    width = panel_inverse.shape[1]
    slab = factor_rows.shape[1]
    assert panels == 2 and factor_rows.shape[2] == width
    row = lax.axis_index("row")
    offset = lax.axis_index("col") * slab
    own1 = row_count - 1
    own0 = row_count - 2

    grow = offset + jnp.arange(slab, dtype=jnp.int32)[:, None]
    gcol = jnp.arange(width, dtype=jnp.int32)[None, :]
    lower = gcol <= grow
    diag_scale = jnp.where(gcol == grow, 0.5, 1.0).astype(jnp.float32)

    f0, f1 = factor_rows[0], factor_rows[1]
    a0, a1 = adjoint_rows[0], adjoint_rows[1]
    inv0, inv1 = panel_inverse[0], panel_inverse[1]

    x1 = tmm(f1, jnp.where(lower, a1, 0.0))
    q1 = lax.psum_scatter(phi_sym(x1), "col", scatter_dimension=0, tiled=True)
    w1 = mm(q1, inv1)
    v1 = lax.psum_scatter(tmm(lax.dynamic_slice_in_dim(inv1, offset, slab, 0), w1), "col",
                          scatter_dimension=0, tiled=True)
    diag1 = jnp.where(lower, v1, 0.0) * diag_scale
    gathered_in, v1 = lax.optimization_barrier((factor_rows, v1))
    full = lax.all_gather(gathered_in, "col", axis=1, tiled=True)
    v1 = row_bcast(v1, own1, list(range(own1)))
    full, v1 = lax.optimization_barrier((full, v1))
    a1_left = a1 - mm(v1, full[1])

    col_adj = mm(a1_left, inv0)
    col_adj = row_bcast(col_adj, own0, list(range(own0)))
    cross = tmm(col_adj, f1)
    x0 = tmm(f0, jnp.where(lower, a0, 0.0)) - tmm(full[0], jnp.tril(cross))
    summed = lax.psum_scatter(jnp.where(row == own0, phi_sym(x0), cross), "col",
                              scatter_dimension=0, tiled=True)
    w0 = mm(summed, inv0)
    v0 = lax.psum_scatter(tmm(lax.dynamic_slice_in_dim(inv0, offset, slab, 0), w0), "col",
                          scatter_dimension=0, tiled=True)
    diag0 = jnp.where(lower, v0, 0.0) * diag_scale
    v0 = row_bcast(v0, own0, list(range(own0)))

    left1 = a1_left - mm(col_adj, full[0])
    left0 = a0 - summed - mm(v0, full[0])
    out1 = jnp.where(row < own0, left1, jnp.where(row == own0, col_adj, diag1))
    out0 = jnp.where(row < own0, left0, jnp.where(row == own0, diag0, a0))
    return jnp.stack([out0, out1])


def solution(mesh):
    return jax.shard_map(
        local,
        mesh=mesh,
        in_specs=(P(None, "col", "row"), P(None, "col", "row"), P()),
        out_specs=P(None, "col", "row"),
        check_vma=False,
    )
```

```python
import jax
import jax.numpy as jnp
from jax import lax
from jax.sharding import PartitionSpec as P

HIGHEST = lax.Precision.HIGHEST


def mm(left, right):
    return jnp.dot(left, right, precision=HIGHEST, preferred_element_type=jnp.float32)


def tmm(left, right):
    return lax.dot_general(left, right, (((0,), (0,)), ((), ())), precision=HIGHEST,
                           preferred_element_type=jnp.float32)


def phi(matrix):
    eye = jnp.eye(matrix.shape[0], dtype=jnp.float32)
    return jnp.tril(matrix) * (1.0 - 0.5 * eye)


def sandwich(lower_half, inverse):
    half = tmm(inverse, mm(lower_half, inverse))
    return half + half.T


def row_bcast(value, source, targets):
    row = lax.axis_index("row")
    recv = None
    for target in targets:
        got = lax.ppermute(value, "row", [(source, target)])
        recv = got if recv is None else recv + got
    if recv is None:
        return value
    return jnp.where(row == source, value, recv)


def local(factor_rows, adjoint_rows, panel_inverse):
    row_count = lax.axis_size("row")
    panels = panel_inverse.shape[0]
    width = panel_inverse.shape[1]
    slab = factor_rows.shape[1]
    assert panels == 2 and factor_rows.shape[2] == width
    row = lax.axis_index("row")
    offset = lax.axis_index("col") * slab
    own1 = row_count - 1
    own0 = row_count - 2

    grow = offset + jnp.arange(slab, dtype=jnp.int32)[:, None]
    gcol = jnp.arange(width, dtype=jnp.int32)[None, :]
    lower = gcol <= grow
    diag_scale = jnp.where(gcol == grow, 0.5, 1.0).astype(jnp.float32)

    f0, f1 = factor_rows[0], factor_rows[1]
    a0, a1 = adjoint_rows[0], adjoint_rows[1]
    inv0, inv1 = panel_inverse[0], panel_inverse[1]

    full1 = lax.all_gather(f1, "col", axis=0, tiled=True)
    part1 = sandwich(phi(tmm(f1, jnp.where(lower, a1, 0.0))), inv1)
    full1, part1 = lax.optimization_barrier((full1, part1))
    v1 = lax.psum_scatter(part1, "col", scatter_dimension=0, tiled=True)
    diag1 = jnp.where(lower, v1, 0.0) * diag_scale
    f0_in, v1 = lax.optimization_barrier((f0, v1))
    full0 = lax.all_gather(f0_in, "col", axis=0, tiled=True)
    v1_near = jnp.where(row == own1, v1, lax.ppermute(v1, "row", [(own1, own0)]))
    a1_left = a1 - mm(v1_near, full1)

    col_adj = mm(a1_left, inv0)
    sent = row_bcast(jnp.stack([v1_near, col_adj]), own0, list(range(own0)))
    x0 = tmm(f0, jnp.where(lower, a0, 0.0)) - tmm(full0, jnp.tril(tmm(col_adj, f1)))
    part0 = sandwich(phi(x0), inv0)
    cross = tmm(sent[1], f1)
    summed = lax.psum_scatter(jnp.where(row == own0, part0, cross), "col",
                              scatter_dimension=0, tiled=True)
    diag0 = jnp.where(lower, summed, 0.0) * diag_scale
    v0 = row_bcast(summed, own0, list(range(own0)))

    left1 = a1 - mm(sent[0], full1) - mm(sent[1], full0)
    left0 = a0 - summed - mm(v0, full0)
    out1 = jnp.where(row < own0, left1, jnp.where(row == own0, col_adj, diag1))
    out0 = jnp.where(row < own0, left0, jnp.where(row == own0, diag0, a0))
    return jnp.stack([out0, out1])


def solution(mesh):
    return jax.shard_map(
        local,
        mesh=mesh,
        in_specs=(P(None, "col", "row"), P(None, "col", "row"), P()),
        out_specs=P(None, "col", "row"),
        check_vma=False,
    )
```

```python
import jax
import jax.numpy as jnp
from jax import lax
from jax.sharding import PartitionSpec as P

HIGHEST = lax.Precision.HIGHEST


def mm(left, right):
    return jnp.dot(left, right, precision=HIGHEST, preferred_element_type=jnp.float32)


def tmm(left, right):
    return lax.dot_general(left, right, (((0,), (0,)), ((), ())), precision=HIGHEST,
                           preferred_element_type=jnp.float32)


def phi(matrix):
    eye = jnp.eye(matrix.shape[0], dtype=jnp.float32)
    return jnp.tril(matrix) * (1.0 - 0.5 * eye)


def sandwich(lower_half, inverse):
    half = tmm(inverse, mm(lower_half, inverse))
    return half + half.T


def row_bcast(value, source, targets):
    row = lax.axis_index("row")
    recv = None
    for target in targets:
        got = lax.ppermute(value, "row", [(source, target)])
        recv = got if recv is None else recv + got
    if recv is None:
        return value
    return jnp.where(row == source, value, recv)


def local(factor_rows, adjoint_rows, panel_inverse):
    row_count = lax.axis_size("row")
    panels = panel_inverse.shape[0]
    width = panel_inverse.shape[1]
    slab = factor_rows.shape[1]
    assert panels == 2 and factor_rows.shape[2] == width
    row = lax.axis_index("row")
    offset = lax.axis_index("col") * slab
    own1 = row_count - 1
    own0 = row_count - 2

    grow = offset + jnp.arange(slab, dtype=jnp.int32)[:, None]
    gcol = jnp.arange(width, dtype=jnp.int32)[None, :]
    lower = gcol <= grow
    diag_scale = jnp.where(gcol == grow, 0.5, 1.0).astype(jnp.float32)

    f0, f1 = factor_rows[0], factor_rows[1]
    a0, a1 = adjoint_rows[0], adjoint_rows[1]
    inv0, inv1 = panel_inverse[0], panel_inverse[1]

    full1 = lax.all_gather(f1, "col", axis=0, tiled=True)
    part1 = sandwich(phi(tmm(f1, jnp.where(lower, a1, 0.0))), inv1)
    full1, part1 = lax.optimization_barrier((full1, part1))
    v1 = lax.psum_scatter(part1, "col", scatter_dimension=0, tiled=True)
    diag1 = jnp.where(lower, v1, 0.0) * diag_scale
    f0_in, v1 = lax.optimization_barrier((f0, v1))
    full0 = lax.all_gather(f0_in, "col", axis=0, tiled=True)
    v1_near = jnp.where(row == own1, v1, lax.ppermute(v1, "row", [(own1, own0)]))
    a1_left = a1 - mm(v1_near, full1)

    col_adj = mm(a1_left, inv0)
    sent = lax.psum(jnp.where(row == own0, jnp.stack([v1_near, col_adj]), 0.0), "row")
    x0 = tmm(f0, jnp.where(lower, a0, 0.0)) - tmm(full0, jnp.tril(tmm(col_adj, f1)))
    part0 = sandwich(phi(x0), inv0)
    cross = tmm(sent[1], f1)
    summed = lax.psum_scatter(jnp.where(row == own0, part0, cross), "col",
                              scatter_dimension=0, tiled=True)
    diag0 = jnp.where(lower, summed, 0.0) * diag_scale
    v0 = row_bcast(summed, own0, list(range(own0)))

    left1 = a1 - mm(sent[0], full1) - mm(sent[1], full0)
    left0 = a0 - summed - mm(v0, full0)
    out1 = jnp.where(row < own0, left1, jnp.where(row == own0, col_adj, diag1))
    out0 = jnp.where(row < own0, left0, jnp.where(row == own0, diag0, a0))
    return jnp.stack([out0, out1])


def solution(mesh):
    return jax.shard_map(
        local,
        mesh=mesh,
        in_specs=(P(None, "col", "row"), P(None, "col", "row"), P()),
        out_specs=P(None, "col", "row"),
        check_vma=False,
    )
```

```python
import jax
import jax.numpy as jnp
from jax import lax
from jax.sharding import PartitionSpec as P

PRECISION = lax.Precision.HIGH


def mm(left, right):
    return jnp.dot(left, right, precision=PRECISION, preferred_element_type=jnp.float32)


def tmm(left, right):
    return lax.dot_general(left, right, (((0,), (0,)), ((), ())), precision=PRECISION,
                           preferred_element_type=jnp.float32)


def phi(matrix):
    eye = jnp.eye(matrix.shape[0], dtype=jnp.float32)
    return jnp.tril(matrix) * (1.0 - 0.5 * eye)


def sandwich(lower_half, inverse):
    half = tmm(inverse, mm(lower_half, inverse))
    return half + half.T


def row_bcast(value, source, targets):
    row = lax.axis_index("row")
    recv = None
    for target in targets:
        got = lax.ppermute(value, "row", [(source, target)])
        recv = got if recv is None else recv + got
    if recv is None:
        return value
    return jnp.where(row == source, value, recv)


def local(factor_rows, adjoint_rows, panel_inverse):
    row_count = lax.axis_size("row")
    panels = panel_inverse.shape[0]
    width = panel_inverse.shape[1]
    slab = factor_rows.shape[1]
    assert panels == 2 and factor_rows.shape[2] == width
    row = lax.axis_index("row")
    offset = lax.axis_index("col") * slab
    own1 = row_count - 1
    own0 = row_count - 2

    grow = offset + jnp.arange(slab, dtype=jnp.int32)[:, None]
    gcol = jnp.arange(width, dtype=jnp.int32)[None, :]
    lower = gcol <= grow
    diag_scale = jnp.where(gcol == grow, 0.5, 1.0).astype(jnp.float32)

    f0, f1 = factor_rows[0], factor_rows[1]
    a0, a1 = adjoint_rows[0], adjoint_rows[1]
    inv0, inv1 = panel_inverse[0], panel_inverse[1]

    full1 = lax.all_gather(f1, "col", axis=0, tiled=True)
    part1 = sandwich(phi(tmm(f1, jnp.where(lower, a1, 0.0))), inv1)
    full1, part1 = lax.optimization_barrier((full1, part1))
    v1 = lax.psum_scatter(part1, "col", scatter_dimension=0, tiled=True)
    diag1 = jnp.where(lower, v1, 0.0) * diag_scale
    f0_in, v1 = lax.optimization_barrier((f0, v1))
    full0 = lax.all_gather(f0_in, "col", axis=0, tiled=True)
    v1_near = jnp.where(row == own1, v1, lax.ppermute(v1, "row", [(own1, own0)]))
    a1_left = a1 - mm(v1_near, full1)

    col_adj = mm(a1_left, inv0)
    sent = lax.psum(jnp.where(row == own0, jnp.stack([v1_near, col_adj]), 0.0), "row")
    x0 = tmm(f0, jnp.where(lower, a0, 0.0)) - tmm(full0, jnp.tril(tmm(col_adj, f1)))
    part0 = sandwich(phi(x0), inv0)
    cross = tmm(sent[1], f1)
    summed = lax.psum_scatter(jnp.where(row == own0, part0, cross), "col",
                              scatter_dimension=0, tiled=True)
    diag0 = jnp.where(lower, summed, 0.0) * diag_scale
    v0 = row_bcast(summed, own0, list(range(own0)))

    left1 = a1 - mm(sent[0], full1) - mm(sent[1], full0)
    left0 = a0 - summed - mm(v0, full0)
    out1 = jnp.where(row < own0, left1, jnp.where(row == own0, col_adj, diag1))
    out0 = jnp.where(row < own0, left0, jnp.where(row == own0, diag0, a0))
    return jnp.stack([out0, out1])


def solution(mesh):
    return jax.shard_map(
        local,
        mesh=mesh,
        in_specs=(P(None, "col", "row"), P(None, "col", "row"), P()),
        out_specs=P(None, "col", "row"),
        check_vma=False,
    )
```

```python
import jax
import jax.numpy as jnp
from jax import lax
from jax.sharding import PartitionSpec as P

PRECISION = lax.Precision.HIGH


def mm(left, right):
    return jnp.dot(left, right, precision=PRECISION, preferred_element_type=jnp.float32)


def tmm(left, right):
    return lax.dot_general(left, right, (((0,), (0,)), ((), ())), precision=PRECISION,
                           preferred_element_type=jnp.float32)


def phi(matrix):
    eye = jnp.eye(matrix.shape[0], dtype=jnp.float32)
    return jnp.tril(matrix) * (1.0 - 0.5 * eye)


def sandwich(lower_half, inverse):
    half = tmm(inverse, mm(lower_half, inverse))
    return half + half.T


def row_bcast(value, source, targets):
    row = lax.axis_index("row")
    recv = None
    for target in targets:
        got = lax.ppermute(value, "row", [(source, target)])
        recv = got if recv is None else recv + got
    if recv is None:
        return value
    return jnp.where(row == source, value, recv)


def col_gather(value):
    count = lax.axis_size("col")
    pieces = [value]
    for shift in range(1, count):
        pieces.append(lax.ppermute(value, "col", [(j, (j + shift) % count) for j in range(count)]))
    stacked = jnp.concatenate(pieces[::-1], axis=0)
    return jnp.roll(stacked, (lax.axis_index("col") + 1) * value.shape[0], axis=0)


def local(factor_rows, adjoint_rows, panel_inverse):
    row_count = lax.axis_size("row")
    panels = panel_inverse.shape[0]
    width = panel_inverse.shape[1]
    slab = factor_rows.shape[1]
    assert panels == 2 and factor_rows.shape[2] == width
    row = lax.axis_index("row")
    offset = lax.axis_index("col") * slab
    own1 = row_count - 1
    own0 = row_count - 2

    grow = offset + jnp.arange(slab, dtype=jnp.int32)[:, None]
    gcol = jnp.arange(width, dtype=jnp.int32)[None, :]
    lower = gcol <= grow
    diag_scale = jnp.where(gcol == grow, 0.5, 1.0).astype(jnp.float32)

    f0, f1 = factor_rows[0], factor_rows[1]
    a0, a1 = adjoint_rows[0], adjoint_rows[1]
    inv0, inv1 = panel_inverse[0], panel_inverse[1]

    full1 = lax.all_gather(f1, "col", axis=0, tiled=True)
    full0 = col_gather(f0)
    part1 = sandwich(phi(tmm(f1, jnp.where(lower, a1, 0.0))), inv1)
    full1, part1 = lax.optimization_barrier((full1, part1))
    v1 = lax.psum_scatter(part1, "col", scatter_dimension=0, tiled=True)
    diag1 = jnp.where(lower, v1, 0.0) * diag_scale
    v1_near = jnp.where(row == own1, v1, lax.ppermute(v1, "row", [(own1, own0)]))
    a1_left = a1 - mm(v1_near, full1)

    col_adj = mm(a1_left, inv0)
    sent = lax.psum(jnp.where(row == own0, jnp.stack([v1_near, col_adj]), 0.0), "row")
    x0 = tmm(f0, jnp.where(lower, a0, 0.0)) - tmm(full0, jnp.tril(tmm(col_adj, f1)))
    part0 = sandwich(phi(x0), inv0)
    cross = tmm(sent[1], f1)
    summed = lax.psum_scatter(jnp.where(row == own0, part0, cross), "col",
                              scatter_dimension=0, tiled=True)
    diag0 = jnp.where(lower, summed, 0.0) * diag_scale
    v0 = row_bcast(summed, own0, list(range(own0)))

    left1 = a1 - mm(sent[0], full1) - mm(sent[1], full0)
    left0 = a0 - summed - mm(v0, full0)
    out1 = jnp.where(row < own0, left1, jnp.where(row == own0, col_adj, diag1))
    out0 = jnp.where(row < own0, left0, jnp.where(row == own0, diag0, a0))
    return jnp.stack([out0, out1])


def solution(mesh):
    return jax.shard_map(
        local,
        mesh=mesh,
        in_specs=(P(None, "col", "row"), P(None, "col", "row"), P()),
        out_specs=P(None, "col", "row"),
        check_vma=False,
    )
```

```python
import jax
import jax.numpy as jnp
from jax import lax
from jax.sharding import PartitionSpec as P

PRECISION = lax.Precision.HIGH


def mm(left, right):
    return jnp.dot(left, right, precision=PRECISION, preferred_element_type=jnp.float32)


def tmm(left, right):
    return lax.dot_general(left, right, (((0,), (0,)), ((), ())), precision=PRECISION,
                           preferred_element_type=jnp.float32)


def phi(matrix):
    eye = jnp.eye(matrix.shape[0], dtype=jnp.float32)
    return jnp.tril(matrix) * (1.0 - 0.5 * eye)


def sandwich(lower_half, inverse):
    half = tmm(inverse, mm(lower_half, inverse))
    return half + half.T


def row_bcast(value, source, targets):
    row = lax.axis_index("row")
    recv = None
    for target in targets:
        got = lax.ppermute(value, "row", [(source, target)])
        recv = got if recv is None else recv + got
    if recv is None:
        return value
    return jnp.where(row == source, value, recv)


def local(factor_rows, adjoint_rows, panel_inverse):
    row_count = lax.axis_size("row")
    panels = panel_inverse.shape[0]
    width = panel_inverse.shape[1]
    slab = factor_rows.shape[1]
    assert panels == 2 and factor_rows.shape[2] == width
    row = lax.axis_index("row")
    offset = lax.axis_index("col") * slab
    own1 = row_count - 1
    own0 = row_count - 2

    grow = offset + jnp.arange(slab, dtype=jnp.int32)[:, None]
    gcol = jnp.arange(width, dtype=jnp.int32)[None, :]
    lower = gcol <= grow
    diag_scale = jnp.where(gcol == grow, 0.5, 1.0).astype(jnp.float32)

    f0, f1 = factor_rows[0], factor_rows[1]
    a0, a1 = adjoint_rows[0], adjoint_rows[1]
    inv0, inv1 = panel_inverse[0], panel_inverse[1]

    full = lax.all_gather(factor_rows, "col", axis=1, tiled=True)
    part1 = sandwich(phi(tmm(f1, jnp.where(lower, a1, 0.0))), inv1)
    full, part1 = lax.optimization_barrier((full, part1))
    full0, full1 = full[0], full[1]
    v1 = lax.psum_scatter(part1, "col", scatter_dimension=0, tiled=True)
    diag1 = jnp.where(lower, v1, 0.0) * diag_scale
    v1_near = jnp.where(row == own1, v1, lax.ppermute(v1, "row", [(own1, own0)]))
    a1_left = a1 - mm(v1_near, full1)

    col_adj = mm(a1_left, inv0)
    sent = lax.psum(jnp.where(row == own0, jnp.stack([v1_near, col_adj]), 0.0), "row")
    x0 = tmm(f0, jnp.where(lower, a0, 0.0)) - tmm(full0, jnp.tril(tmm(col_adj, f1)))
    part0 = sandwich(phi(x0), inv0)
    cross = tmm(sent[1], f1)
    summed = lax.psum_scatter(jnp.where(row == own0, part0, cross), "col",
                              scatter_dimension=0, tiled=True)
    diag0 = jnp.where(lower, summed, 0.0) * diag_scale
    v0 = row_bcast(summed, own0, list(range(own0)))

    left1 = a1 - mm(sent[0], full1) - mm(sent[1], full0)
    left0 = a0 - summed - mm(v0, full0)
    out1 = jnp.where(row < own0, left1, jnp.where(row == own0, col_adj, diag1))
    out0 = jnp.where(row < own0, left0, jnp.where(row == own0, diag0, a0))
    return jnp.stack([out0, out1])


def solution(mesh):
    return jax.shard_map(
        local,
        mesh=mesh,
        in_specs=(P(None, "col", "row"), P(None, "col", "row"), P()),
        out_specs=P(None, "col", "row"),
        check_vma=False,
    )
```

```python
import jax
import jax.numpy as jnp
from jax import lax
from jax.sharding import PartitionSpec as P

PRECISION = lax.Precision.HIGH


def mm(left, right):
    return jnp.dot(left, right, precision=PRECISION, preferred_element_type=jnp.float32)


def tmm(left, right):
    return lax.dot_general(left, right, (((0,), (0,)), ((), ())), precision=PRECISION,
                           preferred_element_type=jnp.float32)


def phi(matrix):
    eye = jnp.eye(matrix.shape[0], dtype=jnp.float32)
    return jnp.tril(matrix) * (1.0 - 0.5 * eye)


def sandwich(lower_half, inverse):
    half = tmm(inverse, mm(lower_half, inverse))
    return half + half.T


def row_bcast(value, source, targets):
    row = lax.axis_index("row")
    recv = None
    for target in targets:
        got = lax.ppermute(value, "row", [(source, target)])
        recv = got if recv is None else recv + got
    if recv is None:
        return value
    return jnp.where(row == source, value, recv)


def local(factor_rows, adjoint_rows, panel_inverse):
    row_count = lax.axis_size("row")
    panels = panel_inverse.shape[0]
    width = panel_inverse.shape[1]
    slab = factor_rows.shape[1]
    assert panels == 2 and factor_rows.shape[2] == width
    row = lax.axis_index("row")
    offset = lax.axis_index("col") * slab
    own1 = row_count - 1
    own0 = row_count - 2

    grow = offset + jnp.arange(slab, dtype=jnp.int32)[:, None]
    gcol = jnp.arange(width, dtype=jnp.int32)[None, :]
    lower = gcol <= grow
    diag_scale = jnp.where(gcol == grow, 0.5, 1.0).astype(jnp.float32)

    f0, f1 = factor_rows[0], factor_rows[1]
    a0, a1 = adjoint_rows[0], adjoint_rows[1]
    inv0, inv1 = panel_inverse[0], panel_inverse[1]

    full1 = lax.all_gather(f1, "col", axis=0, tiled=True)
    part1 = sandwich(phi(tmm(f1, jnp.where(lower, a1, 0.0))), inv1)
    full1, part1 = lax.optimization_barrier((full1, part1))
    v1 = lax.psum_scatter(part1, "col", scatter_dimension=0, tiled=True)
    diag1 = jnp.where(lower, v1, 0.0) * diag_scale
    f0_in, v1 = lax.optimization_barrier((f0, v1))
    full0 = lax.all_gather(f0_in, "col", axis=0, tiled=True)
    v1_near = jnp.where(row == own1, v1, lax.ppermute(v1, "row", [(own1, own0)]))
    a1_left = a1 - mm(v1_near, full1)

    col_adj = mm(a1_left, inv0)
    forward = jnp.stack([v1_near, col_adj])
    received = [lax.ppermute(forward, "row", [(own0, target)]) for target in range(own0)]
    x0 = tmm(f0, jnp.where(lower, a0, 0.0)) - tmm(full0, jnp.tril(tmm(col_adj, f1)))
    part0 = sandwich(phi(x0), inv0)
    received, part0 = lax.optimization_barrier((received, part0))
    sent = sum(received[1:], received[0]) if received else forward
    cross = tmm(sent[1], f1)
    summed = lax.psum_scatter(jnp.where(row == own0, part0, cross), "col",
                              scatter_dimension=0, tiled=True)
    diag0 = jnp.where(lower, summed, 0.0) * diag_scale
    v0 = row_bcast(summed, own0, list(range(own0)))

    left1 = a1 - mm(sent[0], full1) - mm(sent[1], full0)
    left0 = a0 - summed - mm(v0, full0)
    out1 = jnp.where(row < own0, left1, jnp.where(row == own0, col_adj, diag1))
    out0 = jnp.where(row < own0, left0, jnp.where(row == own0, diag0, a0))
    return jnp.stack([out0, out1])


def solution(mesh):
    return jax.shard_map(
        local,
        mesh=mesh,
        in_specs=(P(None, "col", "row"), P(None, "col", "row"), P()),
        out_specs=P(None, "col", "row"),
        check_vma=False,
    )
```

```python
import jax
import jax.numpy as jnp
from jax import lax
from jax.sharding import PartitionSpec as P
from jax.experimental import pallas as pl
from jax.experimental.pallas import tpu as pltpu

PRECISION = lax.Precision.HIGH


def mm(left, right):
    return jnp.dot(left, right, precision=PRECISION, preferred_element_type=jnp.float32)


def tmm(left, right):
    return lax.dot_general(left, right, (((0,), (0,)), ((), ())), precision=PRECISION,
                           preferred_element_type=jnp.float32)


def phi(matrix):
    eye = jnp.eye(matrix.shape[0], dtype=jnp.float32)
    return jnp.tril(matrix) * (1.0 - 0.5 * eye)


def sandwich_half(lower_half, inverse):
    return tmm(inverse, mm(lower_half, inverse))


def _sym_kernel(flag_ref, u_ref, ut_ref, alt_ref, o_ref):
    o_ref[...] = jnp.where(flag_ref[0] != 0, u_ref[...] + ut_ref[...].T, alt_ref[...])


def sym_select(flag, half, other, block=256):
    count = half.shape[0] // block
    spec = pl.BlockSpec((block, block), lambda i, j, f: (i, j))
    spec_t = pl.BlockSpec((block, block), lambda i, j, f: (j, i))
    return pl.pallas_call(
        _sym_kernel,
        grid_spec=pltpu.PrefetchScalarGridSpec(
            num_scalar_prefetch=1, grid=(count, count),
            in_specs=[spec, spec_t, spec], out_specs=spec),
        out_shape=jax.ShapeDtypeStruct(half.shape, half.dtype),
    )(jnp.reshape(flag.astype(jnp.int32), (1,)), half, half, other)


def row_bcast(value, source, targets):
    row = lax.axis_index("row")
    recv = None
    for target in targets:
        got = lax.ppermute(value, "row", [(source, target)])
        recv = got if recv is None else recv + got
    if recv is None:
        return value
    return jnp.where(row == source, value, recv)


def local(factor_rows, adjoint_rows, panel_inverse):
    row_count = lax.axis_size("row")
    panels = panel_inverse.shape[0]
    width = panel_inverse.shape[1]
    slab = factor_rows.shape[1]
    assert panels == 2 and factor_rows.shape[2] == width
    row = lax.axis_index("row")
    offset = lax.axis_index("col") * slab
    own1 = row_count - 1
    own0 = row_count - 2

    grow = offset + jnp.arange(slab, dtype=jnp.int32)[:, None]
    gcol = jnp.arange(width, dtype=jnp.int32)[None, :]
    lower = gcol <= grow
    diag_scale = jnp.where(gcol == grow, 0.5, 1.0).astype(jnp.float32)

    f0, f1 = factor_rows[0], factor_rows[1]
    a0, a1 = adjoint_rows[0], adjoint_rows[1]
    inv0, inv1 = panel_inverse[0], panel_inverse[1]

    full1 = lax.all_gather(f1, "col", axis=0, tiled=True)
    half1 = sandwich_half(phi(tmm(f1, jnp.where(lower, a1, 0.0))), inv1)
    part1 = sym_select(jnp.array(True), half1, half1)
    full1, part1 = lax.optimization_barrier((full1, part1))
    v1 = lax.psum_scatter(part1, "col", scatter_dimension=0, tiled=True)
    diag1 = jnp.where(lower, v1, 0.0) * diag_scale
    f0_in, v1 = lax.optimization_barrier((f0, v1))
    full0 = lax.all_gather(f0_in, "col", axis=0, tiled=True)
    v1_near = jnp.where(row == own1, v1, lax.ppermute(v1, "row", [(own1, own0)]))
    a1_left = a1 - mm(v1_near, full1)

    col_adj = mm(a1_left, inv0)
    forward = jnp.stack([v1_near, col_adj])
    received = [lax.ppermute(forward, "row", [(own0, target)]) for target in range(own0)]
    x0 = tmm(f0, jnp.where(lower, a0, 0.0)) - tmm(full0, jnp.tril(tmm(col_adj, f1)))
    part0 = sandwich_half(phi(x0), inv0)
    received, part0 = lax.optimization_barrier((received, part0))
    sent = sum(received[1:], received[0]) if received else forward
    cross = tmm(sent[1], f1)
    summed = lax.psum_scatter(sym_select(row == own0, part0, cross), "col",
                              scatter_dimension=0, tiled=True)
    diag0 = jnp.where(lower, summed, 0.0) * diag_scale
    v0 = row_bcast(summed, own0, list(range(own0)))

    left1 = a1 - mm(sent[0], full1) - mm(sent[1], full0)
    left0 = a0 - summed - mm(v0, full0)
    out1 = jnp.where(row < own0, left1, jnp.where(row == own0, col_adj, diag1))
    out0 = jnp.where(row < own0, left0, jnp.where(row == own0, diag0, a0))
    return jnp.stack([out0, out1])


def solution(mesh):
    return jax.shard_map(
        local,
        mesh=mesh,
        in_specs=(P(None, "col", "row"), P(None, "col", "row"), P()),
        out_specs=P(None, "col", "row"),
        check_vma=False,
    )
```

```python
import jax
import jax.numpy as jnp
from jax import lax
from jax.sharding import PartitionSpec as P
from jax.experimental import pallas as pl
from jax.experimental.pallas import tpu as pltpu

PRECISION = lax.Precision.HIGH


def mm(left, right):
    return jnp.dot(left, right, precision=PRECISION, preferred_element_type=jnp.float32)


def tmm(left, right):
    return lax.dot_general(left, right, (((0,), (0,)), ((), ())), precision=PRECISION,
                           preferred_element_type=jnp.float32)


def phi(matrix):
    eye = jnp.eye(matrix.shape[0], dtype=jnp.float32)
    return jnp.tril(matrix) * (1.0 - 0.5 * eye)


def sandwich_half(lower_half, inverse):
    return tmm(inverse, mm(lower_half, inverse))


def _sym_kernel(flag_ref, u_ref, ut_ref, alt_ref, o_ref):
    o_ref[...] = jnp.where(flag_ref[0] != 0, u_ref[...] + ut_ref[...].T, alt_ref[...])


def sym_select(flag, half, other, parts=1, block=256):
    size = half.shape[0]
    count = size // block
    per_part = count // parts
    spec = pl.BlockSpec((block, block), lambda i, j, f: (i, j))
    spec_t = pl.BlockSpec((block, block), lambda i, j, f: (j, i))
    out_spec = pl.BlockSpec((None, block, block), lambda i, j, f: (j // per_part, i, j % per_part))
    return pl.pallas_call(
        _sym_kernel,
        grid_spec=pltpu.PrefetchScalarGridSpec(
            num_scalar_prefetch=1, grid=(count, count),
            in_specs=[spec, spec_t, spec], out_specs=out_spec),
        out_shape=jax.ShapeDtypeStruct((parts, size, size // parts), half.dtype),
    )(jnp.reshape(flag.astype(jnp.int32), (1,)), half, half, other)


def row_bcast(value, source, targets):
    row = lax.axis_index("row")
    recv = None
    for target in targets:
        got = lax.ppermute(value, "row", [(source, target)])
        recv = got if recv is None else recv + got
    if recv is None:
        return value
    return jnp.where(row == source, value, recv)


def local(factor_rows, adjoint_rows, panel_inverse):
    row_count = lax.axis_size("row")
    panels = panel_inverse.shape[0]
    width = panel_inverse.shape[1]
    slab = factor_rows.shape[1]
    assert panels == 2 and factor_rows.shape[2] == width
    row = lax.axis_index("row")
    offset = lax.axis_index("col") * slab
    own1 = row_count - 1
    own0 = row_count - 2

    grow = offset + jnp.arange(slab, dtype=jnp.int32)[:, None]
    gcol = jnp.arange(width, dtype=jnp.int32)[None, :]
    lower = gcol <= grow
    diag_scale = jnp.where(gcol == grow, 0.5, 1.0).astype(jnp.float32)

    f0, f1 = factor_rows[0], factor_rows[1]
    a0, a1 = adjoint_rows[0], adjoint_rows[1]
    inv0, inv1 = panel_inverse[0], panel_inverse[1]

    full1 = lax.all_gather(f1, "col", axis=0, tiled=True)
    half1 = sandwich_half(phi(tmm(f1, jnp.where(lower, a1, 0.0))), inv1)
    part1 = sym_select(jnp.array(True), half1, half1)[0]
    full1, part1 = lax.optimization_barrier((full1, part1))
    v1 = lax.psum_scatter(part1, "col", scatter_dimension=0, tiled=True)
    diag1 = jnp.where(lower, v1, 0.0) * diag_scale
    f0_in, v1 = lax.optimization_barrier((f0, v1))
    full0 = lax.all_gather(f0_in, "col", axis=0, tiled=True)
    v1_near = jnp.where(row == own1, v1, lax.ppermute(v1, "row", [(own1, own0)]))
    a1_left = a1 - mm(v1_near, full1)

    col_adj = mm(a1_left, inv0)
    forward = jnp.stack([v1_near, col_adj])
    received = [lax.ppermute(forward, "row", [(own0, target)]) for target in range(own0)]
    x0 = tmm(f0, jnp.where(lower, a0, 0.0)) - tmm(full0, jnp.tril(tmm(col_adj, f1)))
    part0 = sandwich_half(phi(x0), inv0)
    received, part0 = lax.optimization_barrier((received, part0))
    sent = sum(received[1:], received[0]) if received else forward
    cross = tmm(sent[1], f1)
    panels_in = sym_select(row == own0, part0, cross, parts=2)
    summed = []
    v0 = []
    for piece in range(2):
        got = lax.psum_scatter(panels_in[piece], "col", scatter_dimension=0, tiled=True)
        summed.append(got)
        v0.append(row_bcast(got, own0, list(range(own0))))
    summed = jnp.concatenate(summed, axis=1)
    diag0 = jnp.where(lower, summed, 0.0) * diag_scale
    split = width // 2
    v0_term = mm(v0[0], full0[:split]) + mm(v0[1], full0[split:])

    left1 = a1 - mm(sent[0], full1) - mm(sent[1], full0)
    left0 = a0 - summed - v0_term
    out1 = jnp.where(row < own0, left1, jnp.where(row == own0, col_adj, diag1))
    out0 = jnp.where(row < own0, left0, jnp.where(row == own0, diag0, a0))
    return jnp.stack([out0, out1])


def solution(mesh):
    return jax.shard_map(
        local,
        mesh=mesh,
        in_specs=(P(None, "col", "row"), P(None, "col", "row"), P()),
        out_specs=P(None, "col", "row"),
        check_vma=False,
    )
```

```python
import jax
import jax.numpy as jnp
from jax import lax
from jax.sharding import PartitionSpec as P
from jax.experimental import pallas as pl
from jax.experimental.pallas import tpu as pltpu

PRECISION = lax.Precision.HIGH


def mm(left, right):
    return jnp.dot(left, right, precision=PRECISION, preferred_element_type=jnp.float32)


def tmm(left, right):
    return lax.dot_general(left, right, (((0,), (0,)), ((), ())), precision=PRECISION,
                           preferred_element_type=jnp.float32)


def phi(matrix):
    eye = jnp.eye(matrix.shape[0], dtype=jnp.float32)
    return jnp.tril(matrix) * (1.0 - 0.5 * eye)


def sandwich_half(lower_half, inverse):
    return tmm(inverse, mm(lower_half, inverse))


def _sym_kernel(flag_ref, u_ref, ut_ref, alt_ref, o_ref):
    o_ref[...] = jnp.where(flag_ref[0] != 0, u_ref[...] + ut_ref[...].T, alt_ref[...])


def sym_select(flag, half, other, block=256):
    count = half.shape[0] // block
    spec = pl.BlockSpec((block, block), lambda i, j, f: (i, j))
    spec_t = pl.BlockSpec((block, block), lambda i, j, f: (j, i))
    return pl.pallas_call(
        _sym_kernel,
        grid_spec=pltpu.PrefetchScalarGridSpec(
            num_scalar_prefetch=1, grid=(count, count),
            in_specs=[spec, spec_t, spec], out_specs=spec),
        out_shape=jax.ShapeDtypeStruct(half.shape, half.dtype),
    )(jnp.reshape(flag.astype(jnp.int32), (1,)), half, half, other)


def row_bcast(value, source, targets):
    row = lax.axis_index("row")
    recv = None
    for target in targets:
        got = lax.ppermute(value, "row", [(source, target)])
        recv = got if recv is None else recv + got
    if recv is None:
        return value
    return jnp.where(row == source, value, recv)


def col_reduce_scatter(value):
    count = lax.axis_size("col")
    pos = lax.axis_index("col")
    slab = value.shape[0] // count
    buf = value.reshape((count, slab) + value.shape[1:])
    bit = 1
    while bit < count:
        pairs = buf.reshape((buf.shape[0] // 2, 2, slab) + value.shape[1:])
        mine = (pos // bit) % 2
        keep = lax.dynamic_index_in_dim(pairs, mine, axis=1, keepdims=False)
        send = lax.dynamic_index_in_dim(pairs, 1 - mine, axis=1, keepdims=False)
        buf = keep + lax.ppermute(send, "col", [(j, j ^ bit) for j in range(count)])
        bit *= 2
    return buf[0]


def local(factor_rows, adjoint_rows, panel_inverse):
    row_count = lax.axis_size("row")
    panels = panel_inverse.shape[0]
    width = panel_inverse.shape[1]
    slab = factor_rows.shape[1]
    assert panels == 2 and factor_rows.shape[2] == width
    row = lax.axis_index("row")
    offset = lax.axis_index("col") * slab
    own1 = row_count - 1
    own0 = row_count - 2

    grow = offset + jnp.arange(slab, dtype=jnp.int32)[:, None]
    gcol = jnp.arange(width, dtype=jnp.int32)[None, :]
    lower = gcol <= grow
    diag_scale = jnp.where(gcol == grow, 0.5, 1.0).astype(jnp.float32)

    f0, f1 = factor_rows[0], factor_rows[1]
    a0, a1 = adjoint_rows[0], adjoint_rows[1]
    inv0, inv1 = panel_inverse[0], panel_inverse[1]

    full1 = lax.all_gather(f1, "col", axis=0, tiled=True)
    half1 = sandwich_half(phi(tmm(f1, jnp.where(lower, a1, 0.0))), inv1)
    part1 = sym_select(jnp.array(True), half1, half1)
    full1, part1 = lax.optimization_barrier((full1, part1))
    v1 = col_reduce_scatter(part1)
    diag1 = jnp.where(lower, v1, 0.0) * diag_scale
    f0_in, v1 = lax.optimization_barrier((f0, v1))
    full0 = lax.all_gather(f0_in, "col", axis=0, tiled=True)
    v1_near = jnp.where(row == own1, v1, lax.ppermute(v1, "row", [(own1, own0)]))
    a1_left = a1 - mm(v1_near, full1)

    col_adj = mm(a1_left, inv0)
    forward = jnp.stack([v1_near, col_adj])
    received = [lax.ppermute(forward, "row", [(own0, target)]) for target in range(own0)]
    x0 = tmm(f0, jnp.where(lower, a0, 0.0)) - tmm(full0, jnp.tril(tmm(col_adj, f1)))
    part0 = sandwich_half(phi(x0), inv0)
    received, part0 = lax.optimization_barrier((received, part0))
    sent = sum(received[1:], received[0]) if received else forward
    cross = tmm(sent[1], f1)
    summed = col_reduce_scatter(sym_select(row == own0, part0, cross))
    diag0 = jnp.where(lower, summed, 0.0) * diag_scale
    v0 = row_bcast(summed, own0, list(range(own0)))

    left1 = a1 - mm(sent[0], full1) - mm(sent[1], full0)
    left0 = a0 - summed - mm(v0, full0)
    out1 = jnp.where(row < own0, left1, jnp.where(row == own0, col_adj, diag1))
    out0 = jnp.where(row < own0, left0, jnp.where(row == own0, diag0, a0))
    return jnp.stack([out0, out1])


def solution(mesh):
    return jax.shard_map(
        local,
        mesh=mesh,
        in_specs=(P(None, "col", "row"), P(None, "col", "row"), P()),
        out_specs=P(None, "col", "row"),
        check_vma=False,
    )
```

```python
import jax
import jax.numpy as jnp
from jax import lax
from jax.sharding import PartitionSpec as P
from jax.experimental import pallas as pl
from jax.experimental.pallas import tpu as pltpu

PRECISION = lax.Precision.HIGH


def mm(left, right):
    return jnp.dot(left, right, precision=PRECISION, preferred_element_type=jnp.float32)


def tmm(left, right):
    return lax.dot_general(left, right, (((0,), (0,)), ((), ())), precision=PRECISION,
                           preferred_element_type=jnp.float32)


def phi(matrix):
    eye = jnp.eye(matrix.shape[0], dtype=jnp.float32)
    return jnp.tril(matrix) * (1.0 - 0.5 * eye)


def sandwich_half(lower_half, inverse):
    return tmm(inverse, mm(lower_half, inverse))


def _sym_kernel(flag_ref, u_ref, ut_ref, alt_ref, o_ref):
    o_ref[...] = jnp.where(flag_ref[0] != 0, u_ref[...] + ut_ref[...].T, alt_ref[...])


def sym_select(flag, half, other, parts=1, block=256):
    size = half.shape[0]
    count = size // block
    per_part = count // parts
    spec = pl.BlockSpec((block, block), lambda i, j, f: (i, j))
    spec_t = pl.BlockSpec((block, block), lambda i, j, f: (j, i))
    out_spec = pl.BlockSpec((None, block, block), lambda i, j, f: (j // per_part, i, j % per_part))
    return pl.pallas_call(
        _sym_kernel,
        grid_spec=pltpu.PrefetchScalarGridSpec(
            num_scalar_prefetch=1, grid=(count, count),
            in_specs=[spec, spec_t, spec], out_specs=out_spec),
        out_shape=jax.ShapeDtypeStruct((parts, size, size // parts), half.dtype),
    )(jnp.reshape(flag.astype(jnp.int32), (1,)), half, half, other)


def row_bcast(value, source, targets):
    row = lax.axis_index("row")
    recv = None
    for target in targets:
        got = lax.ppermute(value, "row", [(source, target)])
        recv = got if recv is None else recv + got
    if recv is None:
        return value
    return jnp.where(row == source, value, recv)


def col_reduce_scatter(value, order):
    count = lax.axis_size("col")
    pos = lax.axis_index("col")
    bits = count.bit_length() - 1
    slab = value.shape[0] // count
    buf = value.reshape((2,) * bits + (slab,) + value.shape[1:])
    axes = [bits - 1 - b for b in range(bits)]
    for bit in order:
        axis = axes.index(bit)
        mine = (pos >> bit) % 2
        keep = lax.dynamic_index_in_dim(buf, mine, axis=axis, keepdims=False)
        send = lax.dynamic_index_in_dim(buf, 1 - mine, axis=axis, keepdims=False)
        buf = keep + lax.ppermute(send, "col", [(j, j ^ (1 << bit)) for j in range(count)])
        axes.pop(axis)
    return buf


def split_reduce_scatter(panels):
    bits = lax.axis_size("col").bit_length() - 1
    first = list(range(bits))
    second = [0] + list(range(bits - 1, 0, -1))
    return jnp.concatenate(
        [col_reduce_scatter(panels[0], first), col_reduce_scatter(panels[1], second)], axis=1)


def local(factor_rows, adjoint_rows, panel_inverse):
    row_count = lax.axis_size("row")
    panels = panel_inverse.shape[0]
    width = panel_inverse.shape[1]
    slab = factor_rows.shape[1]
    assert panels == 2 and factor_rows.shape[2] == width
    row = lax.axis_index("row")
    offset = lax.axis_index("col") * slab
    own1 = row_count - 1
    own0 = row_count - 2

    grow = offset + jnp.arange(slab, dtype=jnp.int32)[:, None]
    gcol = jnp.arange(width, dtype=jnp.int32)[None, :]
    lower = gcol <= grow
    diag_scale = jnp.where(gcol == grow, 0.5, 1.0).astype(jnp.float32)

    f0, f1 = factor_rows[0], factor_rows[1]
    a0, a1 = adjoint_rows[0], adjoint_rows[1]
    inv0, inv1 = panel_inverse[0], panel_inverse[1]

    full1 = lax.all_gather(f1, "col", axis=0, tiled=True)
    half1 = sandwich_half(phi(tmm(f1, jnp.where(lower, a1, 0.0))), inv1)
    part1 = sym_select(jnp.array(True), half1, half1, parts=2)
    full1, part1 = lax.optimization_barrier((full1, part1))
    v1 = split_reduce_scatter(part1)
    diag1 = jnp.where(lower, v1, 0.0) * diag_scale
    f0_in, v1 = lax.optimization_barrier((f0, v1))
    full0 = lax.all_gather(f0_in, "col", axis=0, tiled=True)
    v1_near = jnp.where(row == own1, v1, lax.ppermute(v1, "row", [(own1, own0)]))
    a1_left = a1 - mm(v1_near, full1)

    col_adj = mm(a1_left, inv0)
    forward = jnp.stack([v1_near, col_adj])
    received = [lax.ppermute(forward, "row", [(own0, target)]) for target in range(own0)]
    x0 = tmm(f0, jnp.where(lower, a0, 0.0)) - tmm(full0, jnp.tril(tmm(col_adj, f1)))
    part0 = sandwich_half(phi(x0), inv0)
    received, part0 = lax.optimization_barrier((received, part0))
    sent = sum(received[1:], received[0]) if received else forward
    cross = tmm(sent[1], f1)
    summed = split_reduce_scatter(sym_select(row == own0, part0, cross, parts=2))
    diag0 = jnp.where(lower, summed, 0.0) * diag_scale
    v0 = row_bcast(summed, own0, list(range(own0)))

    left1 = a1 - mm(sent[0], full1) - mm(sent[1], full0)
    left0 = a0 - summed - mm(v0, full0)
    out1 = jnp.where(row < own0, left1, jnp.where(row == own0, col_adj, diag1))
    out0 = jnp.where(row < own0, left0, jnp.where(row == own0, diag0, a0))
    return jnp.stack([out0, out1])


def solution(mesh):
    return jax.shard_map(
        local,
        mesh=mesh,
        in_specs=(P(None, "col", "row"), P(None, "col", "row"), P()),
        out_specs=P(None, "col", "row"),
        check_vma=False,
    )
```

```python
import jax
import jax.numpy as jnp
from jax import lax
from jax.sharding import PartitionSpec as P
from jax.experimental import pallas as pl
from jax.experimental.pallas import tpu as pltpu

PRECISION = lax.Precision.HIGH


def mm(left, right):
    return jnp.dot(left, right, precision=PRECISION, preferred_element_type=jnp.float32)


def tmm(left, right):
    return lax.dot_general(left, right, (((0,), (0,)), ((), ())), precision=PRECISION,
                           preferred_element_type=jnp.float32)


def phi(matrix):
    eye = jnp.eye(matrix.shape[0], dtype=jnp.float32)
    return jnp.tril(matrix) * (1.0 - 0.5 * eye)


def sandwich_half(lower_half, inverse):
    return tmm(inverse, mm(lower_half, inverse))


def _sym_kernel(flag_ref, u_ref, ut_ref, alt_ref, o_ref):
    o_ref[...] = jnp.where(flag_ref[0] != 0, u_ref[...] + ut_ref[...].T, alt_ref[...])


def _sym_only_kernel(u_ref, ut_ref, o_ref):
    o_ref[...] = u_ref[...] + ut_ref[...].T


def sym_select(flag, half, other, parts=1, block=512):
    size = half.shape[0]
    count = size // block
    per_part = count // parts
    out_shape = jax.ShapeDtypeStruct((parts, size, size // parts), half.dtype)
    if flag is None:
        spec = pl.BlockSpec((block, block), lambda i, j: (i, j))
        spec_t = pl.BlockSpec((block, block), lambda i, j: (j, i))
        out_spec = pl.BlockSpec((None, block, block), lambda i, j: (j // per_part, i, j % per_part))
        return pl.pallas_call(_sym_only_kernel, grid=(count, count), in_specs=[spec, spec_t],
                              out_specs=out_spec, out_shape=out_shape)(half, half)
    spec = pl.BlockSpec((block, block), lambda i, j, f: (i, j))
    spec_t = pl.BlockSpec((block, block), lambda i, j, f: (j, i))
    out_spec = pl.BlockSpec((None, block, block), lambda i, j, f: (j // per_part, i, j % per_part))
    return pl.pallas_call(
        _sym_kernel,
        grid_spec=pltpu.PrefetchScalarGridSpec(
            num_scalar_prefetch=1, grid=(count, count),
            in_specs=[spec, spec_t, spec], out_specs=out_spec),
        out_shape=out_shape,
    )(jnp.reshape(flag.astype(jnp.int32), (1,)), half, half, other)


def row_bcast(value, source, targets):
    row = lax.axis_index("row")
    recv = None
    for target in targets:
        got = lax.ppermute(value, "row", [(source, target)])
        recv = got if recv is None else recv + got
    if recv is None:
        return value
    return jnp.where(row == source, value, recv)


def col_reduce_scatter(value, order):
    count = lax.axis_size("col")
    pos = lax.axis_index("col")
    bits = count.bit_length() - 1
    slab = value.shape[0] // count
    buf = value.reshape((2,) * bits + (slab,) + value.shape[1:])
    axes = [bits - 1 - b for b in range(bits)]
    for bit in order:
        axis = axes.index(bit)
        mine = (pos >> bit) % 2
        keep = lax.dynamic_index_in_dim(buf, mine, axis=axis, keepdims=False)
        send = lax.dynamic_index_in_dim(buf, 1 - mine, axis=axis, keepdims=False)
        buf = keep + lax.ppermute(send, "col", [(j, j ^ (1 << bit)) for j in range(count)])
        axes.pop(axis)
    return buf


def split_reduce_scatter(panels):
    bits = lax.axis_size("col").bit_length() - 1
    first = list(range(bits))
    second = [0] + list(range(bits - 1, 0, -1))
    return jnp.concatenate(
        [col_reduce_scatter(panels[0], first), col_reduce_scatter(panels[1], second)], axis=1)


def local(factor_rows, adjoint_rows, panel_inverse):
    row_count = lax.axis_size("row")
    panels = panel_inverse.shape[0]
    width = panel_inverse.shape[1]
    slab = factor_rows.shape[1]
    assert panels == 2 and factor_rows.shape[2] == width
    row = lax.axis_index("row")
    offset = lax.axis_index("col") * slab
    own1 = row_count - 1
    own0 = row_count - 2

    grow = offset + jnp.arange(slab, dtype=jnp.int32)[:, None]
    gcol = jnp.arange(width, dtype=jnp.int32)[None, :]
    lower = gcol <= grow
    diag_scale = jnp.where(gcol == grow, 0.5, 1.0).astype(jnp.float32)

    f0, f1 = factor_rows[0], factor_rows[1]
    a0, a1 = adjoint_rows[0], adjoint_rows[1]
    inv0, inv1 = panel_inverse[0], panel_inverse[1]

    full1 = lax.all_gather(f1, "col", axis=0, tiled=True)
    half1 = sandwich_half(phi(tmm(f1, jnp.where(lower, a1, 0.0))), inv1)
    part1 = sym_select(None, half1, None, parts=2)
    full1, part1 = lax.optimization_barrier((full1, part1))
    v1 = split_reduce_scatter(part1)
    diag1 = jnp.where(lower, v1, 0.0) * diag_scale
    f0_in, v1 = lax.optimization_barrier((f0, v1))
    full0 = lax.all_gather(f0_in, "col", axis=0, tiled=True)
    v1_near = jnp.where(row == own1, v1, lax.ppermute(v1, "row", [(own1, own0)]))
    a1_left = a1 - mm(v1_near, full1)

    col_adj = mm(a1_left, inv0)
    forward = jnp.stack([v1_near, col_adj])
    received = [lax.ppermute(forward, "row", [(own0, target)]) for target in range(own0)]
    x0 = tmm(f0, jnp.where(lower, a0, 0.0)) - tmm(full0, jnp.tril(tmm(col_adj, f1)))
    part0 = sandwich_half(phi(x0), inv0)
    received, part0 = lax.optimization_barrier((received, part0))
    sent = sum(received[1:], received[0]) if received else forward
    cross = tmm(sent[1], f1)
    summed = split_reduce_scatter(sym_select(row == own0, part0, cross, parts=2))
    diag0 = jnp.where(lower, summed, 0.0) * diag_scale
    v0 = row_bcast(summed, own0, list(range(own0)))

    left1 = a1 - mm(sent[0], full1) - mm(sent[1], full0)
    left0 = a0 - summed - mm(v0, full0)
    out1 = jnp.where(row < own0, left1, jnp.where(row == own0, col_adj, diag1))
    out0 = jnp.where(row < own0, left0, jnp.where(row == own0, diag0, a0))
    return jnp.stack([out0, out1])


def solution(mesh):
    return jax.shard_map(
        local,
        mesh=mesh,
        in_specs=(P(None, "col", "row"), P(None, "col", "row"), P()),
        out_specs=P(None, "col", "row"),
        check_vma=False,
    )
```

```python
import jax
import jax.numpy as jnp
from jax import lax
from jax.sharding import PartitionSpec as P
from jax.experimental import pallas as pl
from jax.experimental.pallas import tpu as pltpu

PRECISION = lax.Precision.HIGH


def mm(left, right):
    return jnp.dot(left, right, precision=PRECISION, preferred_element_type=jnp.float32)


def tmm(left, right):
    return lax.dot_general(left, right, (((0,), (0,)), ((), ())), precision=PRECISION,
                           preferred_element_type=jnp.float32)


def phi(matrix):
    eye = jnp.eye(matrix.shape[0], dtype=jnp.float32)
    return jnp.tril(matrix) * (1.0 - 0.5 * eye)


def sandwich_half(lower_half, inverse):
    return tmm(inverse, mm(lower_half, inverse))


def _sym_kernel(flag_ref, u_ref, ut_ref, alt_ref, o_ref):
    o_ref[...] = jnp.where(flag_ref[0] != 0, u_ref[...] + ut_ref[...].T, alt_ref[...])


def _sym_only_kernel(u_ref, ut_ref, o_ref):
    o_ref[...] = u_ref[...] + ut_ref[...].T


def sym_select(flag, half, other, parts=1, block=512):
    size = half.shape[0]
    count = size // block
    per_part = count // parts
    out_shape = jax.ShapeDtypeStruct((parts, size, size // parts), half.dtype)
    if flag is None:
        spec = pl.BlockSpec((block, block), lambda i, j: (i, j))
        spec_t = pl.BlockSpec((block, block), lambda i, j: (j, i))
        out_spec = pl.BlockSpec((None, block, block), lambda i, j: (j // per_part, i, j % per_part))
        return pl.pallas_call(_sym_only_kernel, grid=(count, count), in_specs=[spec, spec_t],
                              out_specs=out_spec, out_shape=out_shape)(half, half)
    spec = pl.BlockSpec((block, block), lambda i, j, f: (i, j))
    spec_t = pl.BlockSpec((block, block), lambda i, j, f: (j, i))
    out_spec = pl.BlockSpec((None, block, block), lambda i, j, f: (j // per_part, i, j % per_part))
    return pl.pallas_call(
        _sym_kernel,
        grid_spec=pltpu.PrefetchScalarGridSpec(
            num_scalar_prefetch=1, grid=(count, count),
            in_specs=[spec, spec_t, spec], out_specs=out_spec),
        out_shape=out_shape,
    )(jnp.reshape(flag.astype(jnp.int32), (1,)), half, half, other)


def row_bcast(value, source, targets):
    row = lax.axis_index("row")
    recv = None
    for target in targets:
        got = lax.ppermute(value, "row", [(source, target)])
        recv = got if recv is None else recv + got
    if recv is None:
        return value
    return jnp.where(row == source, value, recv)


def col_reduce_scatter(value, order):
    count = lax.axis_size("col")
    pos = lax.axis_index("col")
    bits = count.bit_length() - 1
    slab = value.shape[0] // count
    buf = value.reshape((2,) * bits + (slab,) + value.shape[1:])
    axes = [bits - 1 - b for b in range(bits)]
    for bit in order:
        axis = axes.index(bit)
        mine = (pos >> bit) % 2
        keep = lax.dynamic_index_in_dim(buf, mine, axis=axis, keepdims=False)
        send = lax.dynamic_index_in_dim(buf, 1 - mine, axis=axis, keepdims=False)
        buf = keep + lax.ppermute(send, "col", [(j, j ^ (1 << bit)) for j in range(count)])
        axes.pop(axis)
    return buf


def col_all_gather(value, order):
    count = lax.axis_size("col")
    pos = lax.axis_index("col")
    buf = value
    held = []
    for bit in order:
        mine = (pos >> bit) % 2
        recv = lax.ppermute(buf, "col", [(j, j ^ (1 << bit)) for j in range(count)])
        at = sum(1 for b in held if b > bit)
        buf = jnp.stack([jnp.where(mine == 0, buf, recv), jnp.where(mine == 0, recv, buf)], axis=at)
        held.insert(at, bit)
    return buf.reshape((count * value.shape[0],) + value.shape[1:])


def split_all_gather(value):
    bits = lax.axis_size("col").bit_length() - 1
    half = value.shape[1] // 2
    first = list(range(bits))
    second = [0] + list(range(bits - 1, 0, -1))
    return jnp.concatenate(
        [col_all_gather(value[:, :half], first), col_all_gather(value[:, half:], second)], axis=1)


def split_reduce_scatter(panels):
    bits = lax.axis_size("col").bit_length() - 1
    first = list(range(bits))
    second = [0] + list(range(bits - 1, 0, -1))
    return jnp.concatenate(
        [col_reduce_scatter(panels[0], first), col_reduce_scatter(panels[1], second)], axis=1)


def local(factor_rows, adjoint_rows, panel_inverse):
    row_count = lax.axis_size("row")
    panels = panel_inverse.shape[0]
    width = panel_inverse.shape[1]
    slab = factor_rows.shape[1]
    assert panels == 2 and factor_rows.shape[2] == width
    row = lax.axis_index("row")
    offset = lax.axis_index("col") * slab
    own1 = row_count - 1
    own0 = row_count - 2

    grow = offset + jnp.arange(slab, dtype=jnp.int32)[:, None]
    gcol = jnp.arange(width, dtype=jnp.int32)[None, :]
    lower = gcol <= grow
    diag_scale = jnp.where(gcol == grow, 0.5, 1.0).astype(jnp.float32)

    f0, f1 = factor_rows[0], factor_rows[1]
    a0, a1 = adjoint_rows[0], adjoint_rows[1]
    inv0, inv1 = panel_inverse[0], panel_inverse[1]

    full1 = split_all_gather(f1)
    half1 = sandwich_half(phi(tmm(f1, jnp.where(lower, a1, 0.0))), inv1)
    part1 = sym_select(None, half1, None, parts=2)
    full1, part1 = lax.optimization_barrier((full1, part1))
    v1 = split_reduce_scatter(part1)
    diag1 = jnp.where(lower, v1, 0.0) * diag_scale
    f0_in, v1 = lax.optimization_barrier((f0, v1))
    full0 = split_all_gather(f0_in)
    v1_near = jnp.where(row == own1, v1, lax.ppermute(v1, "row", [(own1, own0)]))
    a1_left = a1 - mm(v1_near, full1)

    col_adj = mm(a1_left, inv0)
    forward = jnp.stack([v1_near, col_adj])
    received = [lax.ppermute(forward, "row", [(own0, target)]) for target in range(own0)]
    x0 = tmm(f0, jnp.where(lower, a0, 0.0)) - tmm(full0, jnp.tril(tmm(col_adj, f1)))
    part0 = sandwich_half(phi(x0), inv0)
    received, part0 = lax.optimization_barrier((received, part0))
    sent = sum(received[1:], received[0]) if received else forward
    cross = tmm(sent[1], f1)
    summed = split_reduce_scatter(sym_select(row == own0, part0, cross, parts=2))
    diag0 = jnp.where(lower, summed, 0.0) * diag_scale
    v0 = row_bcast(summed, own0, list(range(own0)))

    left1 = a1 - mm(sent[0], full1) - mm(sent[1], full0)
    left0 = a0 - summed - mm(v0, full0)
    out1 = jnp.where(row < own0, left1, jnp.where(row == own0, col_adj, diag1))
    out0 = jnp.where(row < own0, left0, jnp.where(row == own0, diag0, a0))
    return jnp.stack([out0, out1])


def solution(mesh):
    return jax.shard_map(
        local,
        mesh=mesh,
        in_specs=(P(None, "col", "row"), P(None, "col", "row"), P()),
        out_specs=P(None, "col", "row"),
        check_vma=False,
    )
```

```python
import jax
import jax.numpy as jnp
from jax import lax
from jax.sharding import PartitionSpec as P
from jax.experimental import pallas as pl
from jax.experimental.pallas import tpu as pltpu

PRECISION = lax.Precision.HIGH


def mm(left, right):
    return jnp.dot(left, right, precision=PRECISION, preferred_element_type=jnp.float32)


def tmm(left, right):
    return lax.dot_general(left, right, (((0,), (0,)), ((), ())), precision=PRECISION,
                           preferred_element_type=jnp.float32)


def phi(matrix):
    eye = jnp.eye(matrix.shape[0], dtype=jnp.float32)
    return jnp.tril(matrix) * (1.0 - 0.5 * eye)


def sandwich_half(lower_half, inverse):
    return tmm(inverse, mm(lower_half, inverse))


def _sym_kernel(flag_ref, u_ref, ut_ref, alt_ref, o_ref):
    o_ref[...] = jnp.where(flag_ref[0] != 0, u_ref[...] + ut_ref[...].T, alt_ref[...])


def _sym_only_kernel(u_ref, ut_ref, o_ref):
    o_ref[...] = u_ref[...] + ut_ref[...].T


def sym_select(flag, half, other, parts=1, block=512):
    size = half.shape[0]
    count = size // block
    per_part = count // parts
    out_shape = jax.ShapeDtypeStruct((parts, size, size // parts), half.dtype)
    if flag is None:
        spec = pl.BlockSpec((block, block), lambda i, j: (i, j))
        spec_t = pl.BlockSpec((block, block), lambda i, j: (j, i))
        out_spec = pl.BlockSpec((None, block, block), lambda i, j: (j // per_part, i, j % per_part))
        return pl.pallas_call(_sym_only_kernel, grid=(count, count), in_specs=[spec, spec_t],
                              out_specs=out_spec, out_shape=out_shape)(half, half)
    spec = pl.BlockSpec((block, block), lambda i, j, f: (i, j))
    spec_t = pl.BlockSpec((block, block), lambda i, j, f: (j, i))
    out_spec = pl.BlockSpec((None, block, block), lambda i, j, f: (j // per_part, i, j % per_part))
    return pl.pallas_call(
        _sym_kernel,
        grid_spec=pltpu.PrefetchScalarGridSpec(
            num_scalar_prefetch=1, grid=(count, count),
            in_specs=[spec, spec_t, spec], out_specs=out_spec),
        out_shape=out_shape,
    )(jnp.reshape(flag.astype(jnp.int32), (1,)), half, half, other)


def row_bcast(value, source, targets):
    row = lax.axis_index("row")
    recv = None
    for target in targets:
        got = lax.ppermute(value, "row", [(source, target)])
        recv = got if recv is None else recv + got
    if recv is None:
        return value
    return jnp.where(row == source, value, recv)


def col_reduce_scatter(value, order):
    count = lax.axis_size("col")
    pos = lax.axis_index("col")
    bits = count.bit_length() - 1
    slab = value.shape[0] // count
    buf = value.reshape((2,) * bits + (slab,) + value.shape[1:])
    axes = [bits - 1 - b for b in range(bits)]
    for bit in order:
        axis = axes.index(bit)
        mine = (pos >> bit) % 2
        keep = lax.dynamic_index_in_dim(buf, mine, axis=axis, keepdims=False)
        send = lax.dynamic_index_in_dim(buf, 1 - mine, axis=axis, keepdims=False)
        buf = keep + lax.ppermute(send, "col", [(j, j ^ (1 << bit)) for j in range(count)])
        axes.pop(axis)
    return buf


def split_reduce_scatter(panels):
    bits = lax.axis_size("col").bit_length() - 1
    first = list(range(bits))
    second = [0] + list(range(bits - 1, 0, -1))
    return jnp.concatenate(
        [col_reduce_scatter(panels[0], first), col_reduce_scatter(panels[1], second)], axis=1)


def local(factor_rows, adjoint_rows, panel_inverse):
    row_count = lax.axis_size("row")
    panels = panel_inverse.shape[0]
    width = panel_inverse.shape[1]
    slab = factor_rows.shape[1]
    assert panels == 2 and factor_rows.shape[2] == width
    row = lax.axis_index("row")
    offset = lax.axis_index("col") * slab
    own1 = row_count - 1
    own0 = row_count - 2

    grow = offset + jnp.arange(slab, dtype=jnp.int32)[:, None]
    gcol = jnp.arange(width, dtype=jnp.int32)[None, :]
    lower = gcol <= grow
    diag_scale = jnp.where(gcol == grow, 0.5, 1.0).astype(jnp.float32)

    f0, f1 = factor_rows[0], factor_rows[1]
    a0, a1 = adjoint_rows[0], adjoint_rows[1]
    inv0, inv1 = panel_inverse[0], panel_inverse[1]

    full1 = lax.all_gather(f1, "col", axis=0, tiled=True)
    half1 = sandwich_half(phi(tmm(f1, jnp.where(lower, a1, 0.0))), inv1)
    part1 = sym_select(None, half1, None, parts=2)
    full1, part1 = lax.optimization_barrier((full1, part1))
    v1 = split_reduce_scatter(part1)
    diag1 = jnp.where(lower, v1, 0.0) * diag_scale
    full0 = lax.all_gather(f0, "col", axis=0, tiled=True)
    v1_near = jnp.where(row == own1, v1, lax.ppermute(v1, "row", [(own1, own0)]))
    a1_left = a1 - mm(v1_near, full1)

    col_adj = mm(a1_left, inv0)
    forward = jnp.stack([v1_near, col_adj])
    received = [lax.ppermute(forward, "row", [(own0, target)]) for target in range(own0)]
    x0 = tmm(f0, jnp.where(lower, a0, 0.0)) - tmm(full0, jnp.tril(tmm(col_adj, f1)))
    part0 = sandwich_half(phi(x0), inv0)
    received, part0 = lax.optimization_barrier((received, part0))
    sent = sum(received[1:], received[0]) if received else forward
    cross = tmm(sent[1], f1)
    summed = split_reduce_scatter(sym_select(row == own0, part0, cross, parts=2))
    diag0 = jnp.where(lower, summed, 0.0) * diag_scale
    v0 = row_bcast(summed, own0, list(range(own0)))

    left1 = a1 - mm(sent[0], full1) - mm(sent[1], full0)
    left0 = a0 - summed - mm(v0, full0)
    out1 = jnp.where(row < own0, left1, jnp.where(row == own0, col_adj, diag1))
    out0 = jnp.where(row < own0, left0, jnp.where(row == own0, diag0, a0))
    return jnp.stack([out0, out1])


def solution(mesh):
    return jax.shard_map(
        local,
        mesh=mesh,
        in_specs=(P(None, "col", "row"), P(None, "col", "row"), P()),
        out_specs=P(None, "col", "row"),
        check_vma=False,
    )
```

```python
import jax
import jax.numpy as jnp
from jax import lax
from jax.sharding import PartitionSpec as P
from jax.experimental import pallas as pl
from jax.experimental.pallas import tpu as pltpu

PRECISION = lax.Precision.HIGHEST


def mm(left, right):
    return jnp.dot(left, right, precision=PRECISION, preferred_element_type=jnp.float32)


def tmm(left, right):
    return lax.dot_general(left, right, (((0,), (0,)), ((), ())), precision=PRECISION,
                           preferred_element_type=jnp.float32)


def phi(matrix):
    eye = jnp.eye(matrix.shape[0], dtype=jnp.float32)
    return jnp.tril(matrix) * (1.0 - 0.5 * eye)


def sandwich_half(lower_half, inverse):
    return tmm(inverse, mm(lower_half, inverse))


def _sym_kernel(flag_ref, u_ref, ut_ref, alt_ref, o_ref):
    o_ref[...] = jnp.where(flag_ref[0] != 0, u_ref[...] + ut_ref[...].T, alt_ref[...])


def _sym_only_kernel(u_ref, ut_ref, o_ref):
    o_ref[...] = u_ref[...] + ut_ref[...].T


def sym_select(flag, half, other, parts=1, block=512):
    size = half.shape[0]
    count = size // block
    per_part = count // parts
    out_shape = jax.ShapeDtypeStruct((parts, size, size // parts), half.dtype)
    if flag is None:
        spec = pl.BlockSpec((block, block), lambda i, j: (i, j))
        spec_t = pl.BlockSpec((block, block), lambda i, j: (j, i))
        out_spec = pl.BlockSpec((None, block, block), lambda i, j: (j // per_part, i, j % per_part))
        return pl.pallas_call(_sym_only_kernel, grid=(count, count), in_specs=[spec, spec_t],
                              out_specs=out_spec, out_shape=out_shape)(half, half)
    spec = pl.BlockSpec((block, block), lambda i, j, f: (i, j))
    spec_t = pl.BlockSpec((block, block), lambda i, j, f: (j, i))
    out_spec = pl.BlockSpec((None, block, block), lambda i, j, f: (j // per_part, i, j % per_part))
    return pl.pallas_call(
        _sym_kernel,
        grid_spec=pltpu.PrefetchScalarGridSpec(
            num_scalar_prefetch=1, grid=(count, count),
            in_specs=[spec, spec_t, spec], out_specs=out_spec),
        out_shape=out_shape,
    )(jnp.reshape(flag.astype(jnp.int32), (1,)), half, half, other)


def row_bcast(value, source, targets):
    row = lax.axis_index("row")
    recv = None
    for target in targets:
        got = lax.ppermute(value, "row", [(source, target)])
        recv = got if recv is None else recv + got
    if recv is None:
        return value
    return jnp.where(row == source, value, recv)


def col_reduce_scatter(value, order):
    count = lax.axis_size("col")
    pos = lax.axis_index("col")
    bits = count.bit_length() - 1
    slab = value.shape[0] // count
    buf = value.reshape((2,) * bits + (slab,) + value.shape[1:])
    axes = [bits - 1 - b for b in range(bits)]
    for bit in order:
        axis = axes.index(bit)
        mine = (pos >> bit) % 2
        keep = lax.dynamic_index_in_dim(buf, mine, axis=axis, keepdims=False)
        send = lax.dynamic_index_in_dim(buf, 1 - mine, axis=axis, keepdims=False)
        buf = keep + lax.ppermute(send, "col", [(j, j ^ (1 << bit)) for j in range(count)])
        axes.pop(axis)
    return buf


def split_reduce_scatter(panels):
    bits = lax.axis_size("col").bit_length() - 1
    first = list(range(bits))
    second = [0] + list(range(bits - 1, 0, -1))
    return jnp.concatenate(
        [col_reduce_scatter(panels[0], first), col_reduce_scatter(panels[1], second)], axis=1)


def local(factor_rows, adjoint_rows, panel_inverse):
    row_count = lax.axis_size("row")
    panels = panel_inverse.shape[0]
    width = panel_inverse.shape[1]
    slab = factor_rows.shape[1]
    assert panels == 2 and factor_rows.shape[2] == width
    row = lax.axis_index("row")
    offset = lax.axis_index("col") * slab
    own1 = row_count - 1
    own0 = row_count - 2

    grow = offset + jnp.arange(slab, dtype=jnp.int32)[:, None]
    gcol = jnp.arange(width, dtype=jnp.int32)[None, :]
    lower = gcol <= grow
    diag_scale = jnp.where(gcol == grow, 0.5, 1.0).astype(jnp.float32)

    f0, f1 = factor_rows[0], factor_rows[1]
    a0, a1 = adjoint_rows[0], adjoint_rows[1]
    inv0, inv1 = panel_inverse[0], panel_inverse[1]

    full1 = lax.all_gather(f1, "col", axis=0, tiled=True)
    half1 = sandwich_half(phi(tmm(f1, jnp.where(lower, a1, 0.0))), inv1)
    part1 = sym_select(None, half1, None, parts=2)
    full1, part1 = lax.optimization_barrier((full1, part1))
    v1 = split_reduce_scatter(part1)
    diag1 = jnp.where(lower, v1, 0.0) * diag_scale
    f0_in, v1 = lax.optimization_barrier((f0, v1))
    full0 = lax.all_gather(f0_in, "col", axis=0, tiled=True)
    v1_near = jnp.where(row == own1, v1, lax.ppermute(v1, "row", [(own1, own0)]))
    a1_left = a1 - mm(v1_near, full1)

    col_adj = mm(a1_left, inv0)
    forward = jnp.stack([v1_near, col_adj])
    received = [lax.ppermute(forward, "row", [(own0, target)]) for target in range(own0)]
    x0 = tmm(f0, jnp.where(lower, a0, 0.0)) - tmm(full0, jnp.tril(tmm(col_adj, f1)))
    part0 = sandwich_half(phi(x0), inv0)
    received, part0 = lax.optimization_barrier((received, part0))
    sent = sum(received[1:], received[0]) if received else forward
    cross = tmm(sent[1], f1)
    summed = split_reduce_scatter(sym_select(row == own0, part0, cross, parts=2))
    diag0 = jnp.where(lower, summed, 0.0) * diag_scale
    v0 = row_bcast(summed, own0, list(range(own0)))

    left1 = a1 - mm(sent[0], full1) - mm(sent[1], full0)
    left0 = a0 - summed - mm(v0, full0)
    out1 = jnp.where(row < own0, left1, jnp.where(row == own0, col_adj, diag1))
    out0 = jnp.where(row < own0, left0, jnp.where(row == own0, diag0, a0))
    return jnp.stack([out0, out1])


def solution(mesh):
    return jax.shard_map(
        local,
        mesh=mesh,
        in_specs=(P(None, "col", "row"), P(None, "col", "row"), P()),
        out_specs=P(None, "col", "row"),
        check_vma=False,
    )
```

```python
import jax
import jax.numpy as jnp
from jax import lax
from jax.sharding import PartitionSpec as P
from jax.experimental import pallas as pl
from jax.experimental.pallas import tpu as pltpu

PRECISION = lax.Precision.HIGHEST


def mm(left, right):
    return jnp.dot(left, right, precision=PRECISION, preferred_element_type=jnp.float32)


def tmm(left, right):
    return lax.dot_general(left, right, (((0,), (0,)), ((), ())), precision=PRECISION,
                           preferred_element_type=jnp.float32)


def phi(matrix):
    eye = jnp.eye(matrix.shape[0], dtype=jnp.float32)
    return jnp.tril(matrix) * (1.0 - 0.5 * eye)


def sandwich_half(lower_half, inverse):
    h = lower_half.shape[0] // 2
    right = jnp.concatenate([mm(lower_half[:h, :h], inverse[:h]), mm(lower_half[h:], inverse)], axis=0)
    return tmm(inverse, right)


def lower_tmm(tri_factor, lower_right):
    h = tri_factor.shape[0] // 2
    top = tmm(tri_factor[:, :h], lower_right[:, :h])
    bottom = tmm(tri_factor[h:, h:], lower_right[h:])
    return jnp.concatenate(
        [jnp.concatenate([top, jnp.zeros_like(top)], axis=1), bottom], axis=0)


def _sym_kernel(flag_ref, u_ref, ut_ref, alt_ref, o_ref):
    o_ref[...] = jnp.where(flag_ref[0] != 0, u_ref[...] + ut_ref[...].T, alt_ref[...])


def _sym_only_kernel(u_ref, ut_ref, o_ref):
    o_ref[...] = u_ref[...] + ut_ref[...].T


def sym_select(flag, half, other, parts=1, block=512):
    size = half.shape[0]
    count = size // block
    per_part = count // parts
    out_shape = jax.ShapeDtypeStruct((parts, size, size // parts), half.dtype)
    if flag is None:
        spec = pl.BlockSpec((block, block), lambda i, j: (i, j))
        spec_t = pl.BlockSpec((block, block), lambda i, j: (j, i))
        out_spec = pl.BlockSpec((None, block, block), lambda i, j: (j // per_part, i, j % per_part))
        return pl.pallas_call(_sym_only_kernel, grid=(count, count), in_specs=[spec, spec_t],
                              out_specs=out_spec, out_shape=out_shape)(half, half)
    spec = pl.BlockSpec((block, block), lambda i, j, f: (i, j))
    spec_t = pl.BlockSpec((block, block), lambda i, j, f: (j, i))
    out_spec = pl.BlockSpec((None, block, block), lambda i, j, f: (j // per_part, i, j % per_part))
    return pl.pallas_call(
        _sym_kernel,
        grid_spec=pltpu.PrefetchScalarGridSpec(
            num_scalar_prefetch=1, grid=(count, count),
            in_specs=[spec, spec_t, spec], out_specs=out_spec),
        out_shape=out_shape,
    )(jnp.reshape(flag.astype(jnp.int32), (1,)), half, half, other)


def row_bcast(value, source, targets):
    row = lax.axis_index("row")
    recv = None
    for target in targets:
        got = lax.ppermute(value, "row", [(source, target)])
        recv = got if recv is None else recv + got
    if recv is None:
        return value
    return jnp.where(row == source, value, recv)


def col_reduce_scatter(value, order):
    count = lax.axis_size("col")
    pos = lax.axis_index("col")
    bits = count.bit_length() - 1
    slab = value.shape[0] // count
    buf = value.reshape((2,) * bits + (slab,) + value.shape[1:])
    axes = [bits - 1 - b for b in range(bits)]
    for bit in order:
        axis = axes.index(bit)
        mine = (pos >> bit) % 2
        keep = lax.dynamic_index_in_dim(buf, mine, axis=axis, keepdims=False)
        send = lax.dynamic_index_in_dim(buf, 1 - mine, axis=axis, keepdims=False)
        buf = keep + lax.ppermute(send, "col", [(j, j ^ (1 << bit)) for j in range(count)])
        axes.pop(axis)
    return buf


def split_reduce_scatter(panels):
    bits = lax.axis_size("col").bit_length() - 1
    first = list(range(bits))
    second = [0] + list(range(bits - 1, 0, -1))
    return jnp.concatenate(
        [col_reduce_scatter(panels[0], first), col_reduce_scatter(panels[1], second)], axis=1)


def local(factor_rows, adjoint_rows, panel_inverse):
    row_count = lax.axis_size("row")
    panels = panel_inverse.shape[0]
    width = panel_inverse.shape[1]
    slab = factor_rows.shape[1]
    assert panels == 2 and factor_rows.shape[2] == width
    row = lax.axis_index("row")
    offset = lax.axis_index("col") * slab
    own1 = row_count - 1
    own0 = row_count - 2

    grow = offset + jnp.arange(slab, dtype=jnp.int32)[:, None]
    gcol = jnp.arange(width, dtype=jnp.int32)[None, :]
    lower = gcol <= grow
    diag_scale = jnp.where(gcol == grow, 0.5, 1.0).astype(jnp.float32)

    f0, f1 = factor_rows[0], factor_rows[1]
    a0, a1 = adjoint_rows[0], adjoint_rows[1]
    inv0, inv1 = panel_inverse[0], panel_inverse[1]

    full1 = lax.all_gather(f1, "col", axis=0, tiled=True)
    half1 = sandwich_half(phi(tmm(f1, jnp.where(lower, a1, 0.0))), inv1)
    part1 = sym_select(None, half1, None, parts=2)
    full1, part1 = lax.optimization_barrier((full1, part1))
    v1 = split_reduce_scatter(part1)
    diag1 = jnp.where(lower, v1, 0.0) * diag_scale
    f0_in, v1 = lax.optimization_barrier((f0, v1))
    full0 = lax.all_gather(f0_in, "col", axis=0, tiled=True)
    v1_near = jnp.where(row == own1, v1, lax.ppermute(v1, "row", [(own1, own0)]))
    a1_left = a1 - mm(v1_near, full1)

    col_adj = mm(a1_left, inv0)
    forward = jnp.stack([v1_near, col_adj])
    received = [lax.ppermute(forward, "row", [(own0, target)]) for target in range(own0)]
    x0 = tmm(f0, jnp.where(lower, a0, 0.0)) - lower_tmm(full0, jnp.tril(tmm(col_adj, f1)))
    part0 = sandwich_half(phi(x0), inv0)
    received, part0 = lax.optimization_barrier((received, part0))
    sent = sum(received[1:], received[0]) if received else forward
    cross = tmm(sent[1], f1)
    summed = split_reduce_scatter(sym_select(row == own0, part0, cross, parts=2))
    diag0 = jnp.where(lower, summed, 0.0) * diag_scale
    v0 = row_bcast(summed, own0, list(range(own0)))

    left1 = a1 - mm(sent[0], full1) - mm(sent[1], full0)
    left0 = a0 - summed - mm(v0, full0)
    out1 = jnp.where(row < own0, left1, jnp.where(row == own0, col_adj, diag1))
    out0 = jnp.where(row < own0, left0, jnp.where(row == own0, diag0, a0))
    return jnp.stack([out0, out1])


def solution(mesh):
    return jax.shard_map(
        local,
        mesh=mesh,
        in_specs=(P(None, "col", "row"), P(None, "col", "row"), P()),
        out_specs=P(None, "col", "row"),
        check_vma=False,
    )
```

```python
import jax
import jax.numpy as jnp
from jax import lax
from jax.sharding import PartitionSpec as P
from jax.experimental import pallas as pl
from jax.experimental.pallas import tpu as pltpu

PRECISION = lax.Precision.HIGHEST


def mm(left, right):
    return jnp.dot(left, right, precision=PRECISION, preferred_element_type=jnp.float32)


def tmm(left, right):
    return lax.dot_general(left, right, (((0,), (0,)), ((), ())), precision=PRECISION,
                           preferred_element_type=jnp.float32)


def phi(matrix):
    eye = jnp.eye(matrix.shape[0], dtype=jnp.float32)
    return jnp.tril(matrix) * (1.0 - 0.5 * eye)


def sandwich_half(lower_half, inverse, split=True):
    if not split:
        return tmm(inverse, mm(lower_half, inverse))
    h = lower_half.shape[0] // 2
    right = jnp.concatenate([mm(lower_half[:h, :h], inverse[:h]), mm(lower_half[h:], inverse)], axis=0)
    return tmm(inverse, right)


def lower_tmm(tri_factor, lower_right):
    h = tri_factor.shape[0] // 2
    top = tmm(tri_factor[:, :h], lower_right[:, :h])
    bottom = tmm(tri_factor[h:, h:], lower_right[h:])
    return jnp.concatenate(
        [jnp.concatenate([top, jnp.zeros_like(top)], axis=1), bottom], axis=0)


def _sym_kernel(flag_ref, u_ref, ut_ref, alt_ref, o_ref):
    o_ref[...] = jnp.where(flag_ref[0] != 0, u_ref[...] + ut_ref[...].T, alt_ref[...])


def _sym_only_kernel(u_ref, ut_ref, o_ref):
    o_ref[...] = u_ref[...] + ut_ref[...].T


def sym_select(flag, half, other, parts=1, block=512):
    size = half.shape[0]
    count = size // block
    per_part = count // parts
    out_shape = jax.ShapeDtypeStruct((parts, size, size // parts), half.dtype)
    if flag is None:
        spec = pl.BlockSpec((block, block), lambda i, j: (i, j))
        spec_t = pl.BlockSpec((block, block), lambda i, j: (j, i))
        out_spec = pl.BlockSpec((None, block, block), lambda i, j: (j // per_part, i, j % per_part))
        return pl.pallas_call(_sym_only_kernel, grid=(count, count), in_specs=[spec, spec_t],
                              out_specs=out_spec, out_shape=out_shape)(half, half)
    spec = pl.BlockSpec((block, block), lambda i, j, f: (i, j))
    spec_t = pl.BlockSpec((block, block), lambda i, j, f: (j, i))
    out_spec = pl.BlockSpec((None, block, block), lambda i, j, f: (j // per_part, i, j % per_part))
    return pl.pallas_call(
        _sym_kernel,
        grid_spec=pltpu.PrefetchScalarGridSpec(
            num_scalar_prefetch=1, grid=(count, count),
            in_specs=[spec, spec_t, spec], out_specs=out_spec),
        out_shape=out_shape,
    )(jnp.reshape(flag.astype(jnp.int32), (1,)), half, half, other)


def row_bcast(value, source, targets):
    row = lax.axis_index("row")
    recv = None
    for target in targets:
        got = lax.ppermute(value, "row", [(source, target)])
        recv = got if recv is None else recv + got
    if recv is None:
        return value
    return jnp.where(row == source, value, recv)


def col_reduce_scatter(value, order):
    count = lax.axis_size("col")
    pos = lax.axis_index("col")
    bits = count.bit_length() - 1
    slab = value.shape[0] // count
    buf = value.reshape((2,) * bits + (slab,) + value.shape[1:])
    axes = [bits - 1 - b for b in range(bits)]
    for bit in order:
        axis = axes.index(bit)
        mine = (pos >> bit) % 2
        keep = lax.dynamic_index_in_dim(buf, mine, axis=axis, keepdims=False)
        send = lax.dynamic_index_in_dim(buf, 1 - mine, axis=axis, keepdims=False)
        buf = keep + lax.ppermute(send, "col", [(j, j ^ (1 << bit)) for j in range(count)])
        axes.pop(axis)
    return buf


def split_reduce_scatter(panels):
    bits = lax.axis_size("col").bit_length() - 1
    first = list(range(bits))
    second = [0] + list(range(bits - 1, 0, -1))
    return jnp.concatenate(
        [col_reduce_scatter(panels[0], first), col_reduce_scatter(panels[1], second)], axis=1)


def local(factor_rows, adjoint_rows, panel_inverse):
    row_count = lax.axis_size("row")
    panels = panel_inverse.shape[0]
    width = panel_inverse.shape[1]
    slab = factor_rows.shape[1]
    assert panels == 2 and factor_rows.shape[2] == width
    row = lax.axis_index("row")
    offset = lax.axis_index("col") * slab
    own1 = row_count - 1
    own0 = row_count - 2

    grow = offset + jnp.arange(slab, dtype=jnp.int32)[:, None]
    gcol = jnp.arange(width, dtype=jnp.int32)[None, :]
    lower = gcol <= grow
    diag_scale = jnp.where(gcol == grow, 0.5, 1.0).astype(jnp.float32)

    f0, f1 = factor_rows[0], factor_rows[1]
    a0, a1 = adjoint_rows[0], adjoint_rows[1]
    inv0, inv1 = panel_inverse[0], panel_inverse[1]

    full1 = lax.all_gather(f1, "col", axis=0, tiled=True)
    half1 = sandwich_half(phi(tmm(f1, jnp.where(lower, a1, 0.0))), inv1, split=False)
    part1 = sym_select(None, half1, None, parts=2)
    full1, part1 = lax.optimization_barrier((full1, part1))
    v1 = split_reduce_scatter(part1)
    diag1 = jnp.where(lower, v1, 0.0) * diag_scale
    f0_in, v1 = lax.optimization_barrier((f0, v1))
    full0 = lax.all_gather(f0_in, "col", axis=0, tiled=True)
    v1_near = jnp.where(row == own1, v1, lax.ppermute(v1, "row", [(own1, own0)]))
    a1_left = a1 - mm(v1_near, full1)

    col_adj = mm(a1_left, inv0)
    forward = jnp.stack([v1_near, col_adj])
    received = [lax.ppermute(forward, "row", [(own0, target)]) for target in range(own0)]
    x0 = tmm(f0, jnp.where(lower, a0, 0.0)) - lower_tmm(full0, jnp.tril(tmm(col_adj, f1)))
    part0 = sandwich_half(phi(x0), inv0)
    received, part0 = lax.optimization_barrier((received, part0))
    sent = sum(received[1:], received[0]) if received else forward
    cross = tmm(sent[1], f1)
    summed = split_reduce_scatter(sym_select(row == own0, part0, cross, parts=2))
    diag0 = jnp.where(lower, summed, 0.0) * diag_scale
    v0 = row_bcast(summed, own0, list(range(own0)))

    left1 = a1 - mm(sent[0], full1) - mm(sent[1], full0)
    left0 = a0 - summed - mm(v0, full0)
    out1 = jnp.where(row < own0, left1, jnp.where(row == own0, col_adj, diag1))
    out0 = jnp.where(row < own0, left0, jnp.where(row == own0, diag0, a0))
    return jnp.stack([out0, out1])


def solution(mesh):
    return jax.shard_map(
        local,
        mesh=mesh,
        in_specs=(P(None, "col", "row"), P(None, "col", "row"), P()),
        out_specs=P(None, "col", "row"),
        check_vma=False,
    )
```

```python
import jax
import jax.numpy as jnp
from jax import lax
from jax.sharding import PartitionSpec as P
from jax.experimental import pallas as pl
from jax.experimental.pallas import tpu as pltpu

PRECISION = lax.Precision.HIGHEST
FAST = lax.Precision.HIGH


def mm(left, right, precision=PRECISION):
    return jnp.dot(left, right, precision=precision, preferred_element_type=jnp.float32)


def tmm(left, right, precision=PRECISION):
    return lax.dot_general(left, right, (((0,), (0,)), ((), ())), precision=precision,
                           preferred_element_type=jnp.float32)


def phi(matrix):
    eye = jnp.eye(matrix.shape[0], dtype=jnp.float32)
    return jnp.tril(matrix) * (1.0 - 0.5 * eye)


def sandwich_half(lower_half, inverse, split=True):
    if not split:
        return tmm(inverse, mm(lower_half, inverse))
    h = lower_half.shape[0] // 2
    right = jnp.concatenate([mm(lower_half[:h, :h], inverse[:h], FAST),
                             mm(lower_half[h:], inverse, FAST)], axis=0)
    return tmm(inverse, right, FAST)


def lower_tmm(tri_factor, lower_right):
    h = tri_factor.shape[0] // 2
    top = tmm(tri_factor[:, :h], lower_right[:, :h], FAST)
    bottom = tmm(tri_factor[h:, h:], lower_right[h:], FAST)
    return jnp.concatenate(
        [jnp.concatenate([top, jnp.zeros_like(top)], axis=1), bottom], axis=0)


def _sym_kernel(flag_ref, u_ref, ut_ref, alt_ref, o_ref):
    o_ref[...] = jnp.where(flag_ref[0] != 0, u_ref[...] + ut_ref[...].T, alt_ref[...])


def _sym_only_kernel(u_ref, ut_ref, o_ref):
    o_ref[...] = u_ref[...] + ut_ref[...].T


def sym_select(flag, half, other, parts=1, block=512):
    size = half.shape[0]
    count = size // block
    per_part = count // parts
    out_shape = jax.ShapeDtypeStruct((parts, size, size // parts), half.dtype)
    if flag is None:
        spec = pl.BlockSpec((block, block), lambda i, j: (i, j))
        spec_t = pl.BlockSpec((block, block), lambda i, j: (j, i))
        out_spec = pl.BlockSpec((None, block, block), lambda i, j: (j // per_part, i, j % per_part))
        return pl.pallas_call(_sym_only_kernel, grid=(count, count), in_specs=[spec, spec_t],
                              out_specs=out_spec, out_shape=out_shape)(half, half)
    spec = pl.BlockSpec((block, block), lambda i, j, f: (i, j))
    spec_t = pl.BlockSpec((block, block), lambda i, j, f: (j, i))
    out_spec = pl.BlockSpec((None, block, block), lambda i, j, f: (j // per_part, i, j % per_part))
    return pl.pallas_call(
        _sym_kernel,
        grid_spec=pltpu.PrefetchScalarGridSpec(
            num_scalar_prefetch=1, grid=(count, count),
            in_specs=[spec, spec_t, spec], out_specs=out_spec),
        out_shape=out_shape,
    )(jnp.reshape(flag.astype(jnp.int32), (1,)), half, half, other)


def row_bcast(value, source, targets):
    row = lax.axis_index("row")
    recv = None
    for target in targets:
        got = lax.ppermute(value, "row", [(source, target)])
        recv = got if recv is None else recv + got
    if recv is None:
        return value
    return jnp.where(row == source, value, recv)


def col_reduce_scatter(value, order):
    count = lax.axis_size("col")
    pos = lax.axis_index("col")
    bits = count.bit_length() - 1
    slab = value.shape[0] // count
    buf = value.reshape((2,) * bits + (slab,) + value.shape[1:])
    axes = [bits - 1 - b for b in range(bits)]
    for bit in order:
        axis = axes.index(bit)
        mine = (pos >> bit) % 2
        keep = lax.dynamic_index_in_dim(buf, mine, axis=axis, keepdims=False)
        send = lax.dynamic_index_in_dim(buf, 1 - mine, axis=axis, keepdims=False)
        buf = keep + lax.ppermute(send, "col", [(j, j ^ (1 << bit)) for j in range(count)])
        axes.pop(axis)
    return buf


def split_reduce_scatter(panels):
    bits = lax.axis_size("col").bit_length() - 1
    first = list(range(bits))
    second = [0] + list(range(bits - 1, 0, -1))
    return jnp.concatenate(
        [col_reduce_scatter(panels[0], first), col_reduce_scatter(panels[1], second)], axis=1)


def local(factor_rows, adjoint_rows, panel_inverse):
    row_count = lax.axis_size("row")
    panels = panel_inverse.shape[0]
    width = panel_inverse.shape[1]
    slab = factor_rows.shape[1]
    assert panels == 2 and factor_rows.shape[2] == width
    row = lax.axis_index("row")
    offset = lax.axis_index("col") * slab
    own1 = row_count - 1
    own0 = row_count - 2

    grow = offset + jnp.arange(slab, dtype=jnp.int32)[:, None]
    gcol = jnp.arange(width, dtype=jnp.int32)[None, :]
    lower = gcol <= grow
    diag_scale = jnp.where(gcol == grow, 0.5, 1.0).astype(jnp.float32)

    f0, f1 = factor_rows[0], factor_rows[1]
    a0, a1 = adjoint_rows[0], adjoint_rows[1]
    inv0, inv1 = panel_inverse[0], panel_inverse[1]

    full1 = lax.all_gather(f1, "col", axis=0, tiled=True)
    half1 = sandwich_half(phi(tmm(f1, jnp.where(lower, a1, 0.0))), inv1, split=False)
    part1 = sym_select(None, half1, None, parts=2)
    full1, part1 = lax.optimization_barrier((full1, part1))
    v1 = split_reduce_scatter(part1)
    diag1 = jnp.where(lower, v1, 0.0) * diag_scale
    f0_in, v1 = lax.optimization_barrier((f0, v1))
    full0 = lax.all_gather(f0_in, "col", axis=0, tiled=True)
    v1_near = jnp.where(row == own1, v1, lax.ppermute(v1, "row", [(own1, own0)]))
    a1_left = a1 - mm(v1_near, full1)

    col_adj = mm(a1_left, inv0)
    forward = jnp.stack([v1_near, col_adj])
    received = [lax.ppermute(forward, "row", [(own0, target)]) for target in range(own0)]
    x0 = tmm(f0, jnp.where(lower, a0, 0.0)) - lower_tmm(full0, jnp.tril(tmm(col_adj, f1)))
    part0 = sandwich_half(phi(x0), inv0)
    received, part0 = lax.optimization_barrier((received, part0))
    sent = sum(received[1:], received[0]) if received else forward
    cross = tmm(sent[1], f1)
    summed = split_reduce_scatter(sym_select(row == own0, part0, cross, parts=2))
    diag0 = jnp.where(lower, summed, 0.0) * diag_scale
    v0 = row_bcast(summed, own0, list(range(own0)))

    left1 = a1 - mm(sent[0], full1) - mm(sent[1], full0)
    left0 = a0 - summed - mm(v0, full0)
    out1 = jnp.where(row < own0, left1, jnp.where(row == own0, col_adj, diag1))
    out0 = jnp.where(row < own0, left0, jnp.where(row == own0, diag0, a0))
    return jnp.stack([out0, out1])


def solution(mesh):
    return jax.shard_map(
        local,
        mesh=mesh,
        in_specs=(P(None, "col", "row"), P(None, "col", "row"), P()),
        out_specs=P(None, "col", "row"),
        check_vma=False,
    )
```

```python
import jax
import jax.numpy as jnp
from jax import lax
from jax.sharding import PartitionSpec as P
from jax.experimental import pallas as pl
from jax.experimental.pallas import tpu as pltpu

PRECISION = lax.Precision.HIGHEST
FAST = lax.Precision.HIGH


def mm(left, right, precision=PRECISION):
    return jnp.dot(left, right, precision=precision, preferred_element_type=jnp.float32)


def tmm(left, right, precision=PRECISION):
    return lax.dot_general(left, right, (((0,), (0,)), ((), ())), precision=precision,
                           preferred_element_type=jnp.float32)


def phi(matrix):
    eye = jnp.eye(matrix.shape[0], dtype=jnp.float32)
    return jnp.tril(matrix) * (1.0 - 0.5 * eye)


def sandwich_half(lower_half, inverse, split=True):
    if not split:
        return tmm(inverse, mm(lower_half, inverse))
    h = lower_half.shape[0] // 2
    right = jnp.concatenate([mm(lower_half[:h, :h], inverse[:h], FAST),
                             mm(lower_half[h:], inverse, FAST)], axis=0)
    return tmm(inverse, right, FAST)


def lower_tmm(tri_factor, lower_right):
    h = tri_factor.shape[0] // 2
    top = tmm(tri_factor[:, :h], lower_right[:, :h], FAST)
    bottom = tmm(tri_factor[h:, h:], lower_right[h:], FAST)
    return jnp.concatenate(
        [jnp.concatenate([top, jnp.zeros_like(top)], axis=1), bottom], axis=0)


def _sym_kernel(flag_ref, u_ref, ut_ref, alt_ref, o_ref):
    o_ref[...] = jnp.where(flag_ref[0] != 0, u_ref[...] + ut_ref[...].T, alt_ref[...])


def _sym_only_kernel(u_ref, ut_ref, o_ref):
    o_ref[...] = u_ref[...] + ut_ref[...].T


def sym_select(flag, half, other, parts=1, block=512):
    size = half.shape[0]
    count = size // block
    per_part = count // parts
    out_shape = jax.ShapeDtypeStruct((parts, size, size // parts), half.dtype)
    if flag is None:
        spec = pl.BlockSpec((block, block), lambda i, j: (i, j))
        spec_t = pl.BlockSpec((block, block), lambda i, j: (j, i))
        out_spec = pl.BlockSpec((None, block, block), lambda i, j: (j // per_part, i, j % per_part))
        return pl.pallas_call(_sym_only_kernel, grid=(count, count), in_specs=[spec, spec_t],
                              out_specs=out_spec, out_shape=out_shape)(half, half)
    spec = pl.BlockSpec((block, block), lambda i, j, f: (i, j))
    spec_t = pl.BlockSpec((block, block), lambda i, j, f: (j, i))
    out_spec = pl.BlockSpec((None, block, block), lambda i, j, f: (j // per_part, i, j % per_part))
    return pl.pallas_call(
        _sym_kernel,
        grid_spec=pltpu.PrefetchScalarGridSpec(
            num_scalar_prefetch=1, grid=(count, count),
            in_specs=[spec, spec_t, spec], out_specs=out_spec),
        out_shape=out_shape,
    )(jnp.reshape(flag.astype(jnp.int32), (1,)), half, half, other)


def row_bcast(value, source, targets):
    row = lax.axis_index("row")
    recv = None
    for target in targets:
        got = lax.ppermute(value, "row", [(source, target)])
        recv = got if recv is None else recv + got
    if recv is None:
        return value
    return jnp.where(row == source, value, recv)


def col_reduce_scatter(value, order):
    count = lax.axis_size("col")
    pos = lax.axis_index("col")
    bits = count.bit_length() - 1
    slab = value.shape[0] // count
    buf = value.reshape((2,) * bits + (slab,) + value.shape[1:])
    axes = [bits - 1 - b for b in range(bits)]
    for bit in order:
        axis = axes.index(bit)
        mine = (pos >> bit) % 2
        keep = lax.dynamic_index_in_dim(buf, mine, axis=axis, keepdims=False)
        send = lax.dynamic_index_in_dim(buf, 1 - mine, axis=axis, keepdims=False)
        buf = keep + lax.ppermute(send, "col", [(j, j ^ (1 << bit)) for j in range(count)])
        axes.pop(axis)
    return buf


def split_reduce_scatter(panels):
    bits = lax.axis_size("col").bit_length() - 1
    first = list(range(bits))
    second = [0] + list(range(bits - 1, 0, -1))
    return jnp.concatenate(
        [col_reduce_scatter(panels[0], first), col_reduce_scatter(panels[1], second)], axis=1)


def local(factor_rows, adjoint_rows, panel_inverse):
    row_count = lax.axis_size("row")
    panels = panel_inverse.shape[0]
    width = panel_inverse.shape[1]
    slab = factor_rows.shape[1]
    assert panels == 2 and factor_rows.shape[2] == width
    row = lax.axis_index("row")
    offset = lax.axis_index("col") * slab
    own1 = row_count - 1
    own0 = row_count - 2

    grow = offset + jnp.arange(slab, dtype=jnp.int32)[:, None]
    gcol = jnp.arange(width, dtype=jnp.int32)[None, :]
    lower = gcol <= grow
    diag_scale = jnp.where(gcol == grow, 0.5, 1.0).astype(jnp.float32)

    f0, f1 = factor_rows[0], factor_rows[1]
    a0, a1 = adjoint_rows[0], adjoint_rows[1]
    inv0, inv1 = panel_inverse[0], panel_inverse[1]

    full1 = lax.all_gather(f1, "col", axis=0, tiled=True)
    half1 = sandwich_half(phi(tmm(f1, jnp.where(lower, a1, 0.0))), inv1, split=False)
    part1 = sym_select(None, half1, None, parts=2)
    full1, part1 = lax.optimization_barrier((full1, part1))
    v1 = split_reduce_scatter(part1)
    diag1 = jnp.where(lower, v1, 0.0) * diag_scale
    f0_in, v1 = lax.optimization_barrier((f0, v1))
    full0 = lax.all_gather(f0_in, "col", axis=0, tiled=True)
    v1_near = jnp.where(row == own1, v1, lax.ppermute(v1, "row", [(own1, own0)]))
    a1_left = a1 - mm(v1_near, full1)

    col_adj = mm(a1_left, inv0)
    col_recv = [lax.ppermute(col_adj, "row", [(own0, target)]) for target in range(own0)]
    col_sent = sum(col_recv[1:], col_recv[0]) if col_recv else col_adj
    cross = tmm(col_sent, f1)
    v1_recv = [lax.ppermute(v1_near, "row", [(own0, target)]) for target in range(own0)]
    x0 = tmm(f0, jnp.where(lower, a0, 0.0)) - lower_tmm(full0, jnp.tril(tmm(col_adj, f1)))
    part0 = sandwich_half(phi(x0), inv0)
    v1_recv, part0 = lax.optimization_barrier((v1_recv, part0))
    v1_sent = sum(v1_recv[1:], v1_recv[0]) if v1_recv else v1_near

    summed = split_reduce_scatter(sym_select(row == own0, part0, cross, parts=2))
    diag0 = jnp.where(lower, summed, 0.0) * diag_scale
    v0 = row_bcast(summed, own0, list(range(own0)))

    left1 = a1 - mm(v1_sent, full1) - mm(col_sent, full0)
    left0 = a0 - summed - mm(v0, full0)
    out1 = jnp.where(row < own0, left1, jnp.where(row == own0, col_adj, diag1))
    out0 = jnp.where(row < own0, left0, jnp.where(row == own0, diag0, a0))
    return jnp.stack([out0, out1])


def solution(mesh):
    return jax.shard_map(
        local,
        mesh=mesh,
        in_specs=(P(None, "col", "row"), P(None, "col", "row"), P()),
        out_specs=P(None, "col", "row"),
        check_vma=False,
    )
```

```python
import jax
import jax.numpy as jnp
from jax import lax
from jax.sharding import PartitionSpec as P
from jax.experimental import pallas as pl
from jax.experimental.pallas import tpu as pltpu

PRECISION = lax.Precision.HIGHEST
FAST = lax.Precision.HIGH


def mm(left, right, precision=PRECISION):
    return jnp.dot(left, right, precision=precision, preferred_element_type=jnp.float32)


def tmm(left, right, precision=PRECISION):
    return lax.dot_general(left, right, (((0,), (0,)), ((), ())), precision=precision,
                           preferred_element_type=jnp.float32)


def phi(matrix):
    eye = jnp.eye(matrix.shape[0], dtype=jnp.float32)
    return jnp.tril(matrix) * (1.0 - 0.5 * eye)


def sandwich_half(lower_half, inverse, split=True):
    if not split:
        return tmm(inverse, mm(lower_half, inverse))
    h = lower_half.shape[0] // 2
    right = jnp.concatenate([mm(lower_half[:h, :h], inverse[:h], FAST),
                             mm(lower_half[h:], inverse, FAST)], axis=0)
    return tmm(inverse, right, FAST)


def lower_tmm(tri_factor, lower_right):
    h = tri_factor.shape[0] // 2
    top = tmm(tri_factor[:, :h], lower_right[:, :h], FAST)
    bottom = tmm(tri_factor[h:, h:], lower_right[h:], FAST)
    return jnp.concatenate(
        [jnp.concatenate([top, jnp.zeros_like(top)], axis=1), bottom], axis=0)


def _sym_kernel(flag_ref, u_ref, ut_ref, alt_ref, o_ref):
    o_ref[...] = jnp.where(flag_ref[0] != 0, u_ref[...] + ut_ref[...].T, alt_ref[...])


def _sym_only_kernel(u_ref, ut_ref, o_ref):
    o_ref[...] = u_ref[...] + ut_ref[...].T


def sym_select(flag, half, other, parts=1, block=512):
    size = half.shape[0]
    count = size // block
    per_part = count // parts
    out_shape = jax.ShapeDtypeStruct((parts, size, size // parts), half.dtype)
    if flag is None:
        spec = pl.BlockSpec((block, block), lambda i, j: (i, j))
        spec_t = pl.BlockSpec((block, block), lambda i, j: (j, i))
        out_spec = pl.BlockSpec((None, block, block), lambda i, j: (j // per_part, i, j % per_part))
        return pl.pallas_call(_sym_only_kernel, grid=(count, count), in_specs=[spec, spec_t],
                              out_specs=out_spec, out_shape=out_shape)(half, half)
    spec = pl.BlockSpec((block, block), lambda i, j, f: (i, j))
    spec_t = pl.BlockSpec((block, block), lambda i, j, f: (j, i))
    out_spec = pl.BlockSpec((None, block, block), lambda i, j, f: (j // per_part, i, j % per_part))
    return pl.pallas_call(
        _sym_kernel,
        grid_spec=pltpu.PrefetchScalarGridSpec(
            num_scalar_prefetch=1, grid=(count, count),
            in_specs=[spec, spec_t, spec], out_specs=out_spec),
        out_shape=out_shape,
    )(jnp.reshape(flag.astype(jnp.int32), (1,)), half, half, other)


def row_bcast(value, source, targets):
    row = lax.axis_index("row")
    recv = None
    for target in targets:
        got = lax.ppermute(value, "row", [(source, target)])
        recv = got if recv is None else recv + got
    if recv is None:
        return value
    return jnp.where(row == source, value, recv)


def col_reduce_scatter(value, order):
    count = lax.axis_size("col")
    pos = lax.axis_index("col")
    bits = count.bit_length() - 1
    slab = value.shape[0] // count
    buf = value.reshape((2,) * bits + (slab,) + value.shape[1:])
    axes = [bits - 1 - b for b in range(bits)]
    for bit in order:
        axis = axes.index(bit)
        mine = (pos >> bit) % 2
        keep = lax.dynamic_index_in_dim(buf, mine, axis=axis, keepdims=False)
        send = lax.dynamic_index_in_dim(buf, 1 - mine, axis=axis, keepdims=False)
        buf = keep + lax.ppermute(send, "col", [(j, j ^ (1 << bit)) for j in range(count)])
        axes.pop(axis)
    return buf


def split_reduce_scatter(panels):
    bits = lax.axis_size("col").bit_length() - 1
    first = list(range(bits))
    second = [0] + list(range(bits - 1, 0, -1))
    return jnp.concatenate(
        [col_reduce_scatter(panels[0], first), col_reduce_scatter(panels[1], second)], axis=1)


def local(factor_rows, adjoint_rows, panel_inverse):
    row_count = lax.axis_size("row")
    panels = panel_inverse.shape[0]
    width = panel_inverse.shape[1]
    slab = factor_rows.shape[1]
    assert panels == 2 and factor_rows.shape[2] == width
    row = lax.axis_index("row")
    offset = lax.axis_index("col") * slab
    own1 = row_count - 1
    own0 = row_count - 2

    grow = offset + jnp.arange(slab, dtype=jnp.int32)[:, None]
    gcol = jnp.arange(width, dtype=jnp.int32)[None, :]
    lower = gcol <= grow
    diag_scale = jnp.where(gcol == grow, 0.5, 1.0).astype(jnp.float32)

    f0, f1 = factor_rows[0], factor_rows[1]
    a0, a1 = adjoint_rows[0], adjoint_rows[1]
    inv0, inv1 = panel_inverse[0], panel_inverse[1]

    full1 = lax.all_gather(f1, "col", axis=0, tiled=True)
    half1 = sandwich_half(phi(tmm(f1, jnp.where(lower, a1, 0.0))), inv1, split=False)
    part1 = sym_select(None, half1, None, parts=2)
    full1, part1 = lax.optimization_barrier((full1, part1))
    v1 = split_reduce_scatter(part1)
    diag1 = jnp.where(lower, v1, 0.0) * diag_scale
    f0_in, v1 = lax.optimization_barrier((f0, v1))
    full0 = lax.all_gather(f0_in, "col", axis=0, tiled=True)
    v1_near = jnp.where(row == own1, v1, lax.ppermute(v1, "row", [(own1, own0)]))
    a1_left = a1 - mm(v1_near, full1)

    col_adj = mm(a1_left, inv0)
    col_recv = [lax.ppermute(col_adj, "row", [(own0, target)]) for target in range(own0)]
    col_sent = sum(col_recv[1:], col_recv[0]) if col_recv else col_adj
    v1_next, col_sent = lax.optimization_barrier((v1_near, col_sent))
    v1_recv = [lax.ppermute(v1_next, "row", [(own0, target)]) for target in range(own0)]
    cross = tmm(col_sent, f1)
    x0 = tmm(f0, jnp.where(lower, a0, 0.0)) - lower_tmm(full0, jnp.tril(tmm(col_adj, f1)))
    part0 = sandwich_half(phi(x0), inv0)
    v1_recv, part0 = lax.optimization_barrier((v1_recv, part0))
    v1_sent = sum(v1_recv[1:], v1_recv[0]) if v1_recv else v1_near

    summed = split_reduce_scatter(sym_select(row == own0, part0, cross, parts=2))
    diag0 = jnp.where(lower, summed, 0.0) * diag_scale
    v0 = row_bcast(summed, own0, list(range(own0)))

    left1 = a1 - mm(v1_sent, full1) - mm(col_sent, full0)
    left0 = a0 - summed - mm(v0, full0)
    out1 = jnp.where(row < own0, left1, jnp.where(row == own0, col_adj, diag1))
    out0 = jnp.where(row < own0, left0, jnp.where(row == own0, diag0, a0))
    return jnp.stack([out0, out1])


def solution(mesh):
    return jax.shard_map(
        local,
        mesh=mesh,
        in_specs=(P(None, "col", "row"), P(None, "col", "row"), P()),
        out_specs=P(None, "col", "row"),
        check_vma=False,
    )
```

```python
import jax
import jax.numpy as jnp
from jax import lax
from jax.sharding import PartitionSpec as P
from jax.experimental import pallas as pl
from jax.experimental.pallas import tpu as pltpu

PRECISION = lax.Precision.HIGHEST
FAST = lax.Precision.HIGH


def mm(left, right, precision=PRECISION):
    return jnp.dot(left, right, precision=precision, preferred_element_type=jnp.float32)


def tmm(left, right, precision=PRECISION):
    return lax.dot_general(left, right, (((0,), (0,)), ((), ())), precision=precision,
                           preferred_element_type=jnp.float32)


def phi(matrix):
    eye = jnp.eye(matrix.shape[0], dtype=jnp.float32)
    return jnp.tril(matrix) * (1.0 - 0.5 * eye)


def sandwich_half(lower_half, inverse, split=True):
    if not split:
        return tmm(inverse, mm(lower_half, inverse))
    h = lower_half.shape[0] // 2
    right = jnp.concatenate([mm(lower_half[:h, :h], inverse[:h], FAST),
                             mm(lower_half[h:], inverse, FAST)], axis=0)
    return tmm(inverse, right, FAST)


def lower_tmm(tri_factor, lower_right):
    h = tri_factor.shape[0] // 2
    top = tmm(tri_factor[:, :h], lower_right[:, :h], FAST)
    bottom = tmm(tri_factor[h:, h:], lower_right[h:], FAST)
    return jnp.concatenate(
        [jnp.concatenate([top, jnp.zeros_like(top)], axis=1), bottom], axis=0)


def _sym_kernel(flag_ref, u_ref, ut_ref, alt_ref, o_ref):
    o_ref[...] = jnp.where(flag_ref[0] != 0, u_ref[...] + ut_ref[...].T, alt_ref[...])


def _sym_only_kernel(u_ref, ut_ref, o_ref):
    o_ref[...] = u_ref[...] + ut_ref[...].T


def sym_select(flag, half, other, parts=1, block=512):
    size = half.shape[0]
    count = size // block
    per_part = count // parts
    out_shape = jax.ShapeDtypeStruct((parts, size, size // parts), half.dtype)
    if flag is None:
        spec = pl.BlockSpec((block, block), lambda i, j: (i, j))
        spec_t = pl.BlockSpec((block, block), lambda i, j: (j, i))
        out_spec = pl.BlockSpec((None, block, block), lambda i, j: (j // per_part, i, j % per_part))
        return pl.pallas_call(_sym_only_kernel, grid=(count, count), in_specs=[spec, spec_t],
                              out_specs=out_spec, out_shape=out_shape)(half, half)
    spec = pl.BlockSpec((block, block), lambda i, j, f: (i, j))
    spec_t = pl.BlockSpec((block, block), lambda i, j, f: (j, i))
    out_spec = pl.BlockSpec((None, block, block), lambda i, j, f: (j // per_part, i, j % per_part))
    return pl.pallas_call(
        _sym_kernel,
        grid_spec=pltpu.PrefetchScalarGridSpec(
            num_scalar_prefetch=1, grid=(count, count),
            in_specs=[spec, spec_t, spec], out_specs=out_spec),
        out_shape=out_shape,
    )(jnp.reshape(flag.astype(jnp.int32), (1,)), half, half, other)


def row_bcast(value, source, targets):
    row = lax.axis_index("row")
    recv = None
    for target in targets:
        got = lax.ppermute(value, "row", [(source, target)])
        recv = got if recv is None else recv + got
    if recv is None:
        return value
    return jnp.where(row == source, value, recv)


def col_reduce_scatter(value, order):
    count = lax.axis_size("col")
    pos = lax.axis_index("col")
    bits = count.bit_length() - 1
    slab = value.shape[0] // count
    buf = value.reshape((2,) * bits + (slab,) + value.shape[1:])
    axes = [bits - 1 - b for b in range(bits)]
    for bit in order:
        axis = axes.index(bit)
        mine = (pos >> bit) % 2
        keep = lax.dynamic_index_in_dim(buf, mine, axis=axis, keepdims=False)
        send = lax.dynamic_index_in_dim(buf, 1 - mine, axis=axis, keepdims=False)
        buf = keep + lax.ppermute(send, "col", [(j, j ^ (1 << bit)) for j in range(count)])
        axes.pop(axis)
    return buf


def split_reduce_scatter(panels):
    bits = lax.axis_size("col").bit_length() - 1
    first = list(range(bits))
    second = [0] + list(range(bits - 1, 0, -1))
    return jnp.concatenate(
        [col_reduce_scatter(panels[0], first), col_reduce_scatter(panels[1], second)], axis=1)


def local(factor_rows, adjoint_rows, panel_inverse):
    row_count = lax.axis_size("row")
    panels = panel_inverse.shape[0]
    width = panel_inverse.shape[1]
    slab = factor_rows.shape[1]
    assert panels == 2 and factor_rows.shape[2] == width
    row = lax.axis_index("row")
    offset = lax.axis_index("col") * slab
    own1 = row_count - 1
    own0 = row_count - 2

    grow = offset + jnp.arange(slab, dtype=jnp.int32)[:, None]
    gcol = jnp.arange(width, dtype=jnp.int32)[None, :]
    lower = gcol <= grow
    diag_scale = jnp.where(gcol == grow, 0.5, 1.0).astype(jnp.float32)

    f0, f1 = factor_rows[0], factor_rows[1]
    a0, a1 = adjoint_rows[0], adjoint_rows[1]
    inv0, inv1 = panel_inverse[0], panel_inverse[1]

    full1 = lax.all_gather(f1, "col", axis=0, tiled=True)
    half1 = sandwich_half(phi(tmm(f1, jnp.where(lower, a1, 0.0))), inv1, split=False)
    part1 = sym_select(None, half1, None, parts=2)
    full1, part1 = lax.optimization_barrier((full1, part1))
    v1 = split_reduce_scatter(part1)
    diag1 = jnp.where(lower, v1, 0.0) * diag_scale
    f0_in, v1 = lax.optimization_barrier((f0, v1))
    full0 = lax.all_gather(f0_in, "col", axis=0, tiled=True)
    v1_near = jnp.where(row == own1, v1, lax.ppermute(v1, "row", [(own1, own0)]))
    a1_left = a1 - mm(v1_near, full1)

    col_adj = mm(a1_left, inv0)
    forward = jnp.stack([v1_near, col_adj])
    received = [lax.ppermute(forward, "row", [(own0, target)]) for target in range(own0)]
    x0 = tmm(f0, jnp.where(lower, a0, 0.0)) - lower_tmm(full0, jnp.tril(tmm(col_adj, f1)))
    part0 = sandwich_half(phi(x0), inv0)
    received, part0 = lax.optimization_barrier((received, part0))
    sent = sum(received[1:], received[0]) if received else forward
    cross = tmm(sent[1], f1, FAST)
    summed = split_reduce_scatter(sym_select(row == own0, part0, cross, parts=2))
    diag0 = jnp.where(lower, summed, 0.0) * diag_scale
    v0 = row_bcast(summed, own0, list(range(own0)))

    left1 = a1 - mm(sent[0], full1) - mm(sent[1], full0)
    left0 = a0 - summed - mm(v0, full0)
    out1 = jnp.where(row < own0, left1, jnp.where(row == own0, col_adj, diag1))
    out0 = jnp.where(row < own0, left0, jnp.where(row == own0, diag0, a0))
    return jnp.stack([out0, out1])


def solution(mesh):
    return jax.shard_map(
        local,
        mesh=mesh,
        in_specs=(P(None, "col", "row"), P(None, "col", "row"), P()),
        out_specs=P(None, "col", "row"),
        check_vma=False,
    )
```

```python
import jax
import jax.numpy as jnp
from jax import lax
from jax.sharding import PartitionSpec as P
from jax.experimental import pallas as pl
from jax.experimental.pallas import tpu as pltpu

PRECISION = lax.Precision.HIGHEST
FAST = lax.Precision.HIGH


def mm(left, right, precision=PRECISION):
    return jnp.dot(left, right, precision=precision, preferred_element_type=jnp.float32)


def tmm(left, right, precision=PRECISION):
    return lax.dot_general(left, right, (((0,), (0,)), ((), ())), precision=precision,
                           preferred_element_type=jnp.float32)


def phi(matrix):
    eye = jnp.eye(matrix.shape[0], dtype=jnp.float32)
    return jnp.tril(matrix) * (1.0 - 0.5 * eye)


def sandwich_half(lower_half, inverse, split=True):
    if not split:
        return tmm(inverse, mm(lower_half, inverse))
    h = lower_half.shape[0] // 2
    right = jnp.concatenate([mm(lower_half[:h, :h], inverse[:h], FAST),
                             mm(lower_half[h:], inverse, FAST)], axis=0)
    return tmm(inverse, right, FAST)


def lower_tmm(tri_factor, lower_right):
    h = tri_factor.shape[0] // 2
    top = tmm(tri_factor[:, :h], lower_right[:, :h], FAST)
    bottom = tmm(tri_factor[h:, h:], lower_right[h:], FAST)
    return jnp.concatenate(
        [jnp.concatenate([top, jnp.zeros_like(top)], axis=1), bottom], axis=0)


def _sym_kernel(flag_ref, u_ref, ut_ref, alt_ref, o_ref):
    o_ref[...] = jnp.where(flag_ref[0] != 0, u_ref[...] + ut_ref[...].T, alt_ref[...])


def _sym_only_kernel(u_ref, ut_ref, o_ref):
    o_ref[...] = u_ref[...] + ut_ref[...].T


def sym_select(flag, half, other, parts=1, block=512):
    size = half.shape[0]
    count = size // block
    per_part = count // parts
    out_shape = jax.ShapeDtypeStruct((parts, size, size // parts), half.dtype)
    if flag is None:
        spec = pl.BlockSpec((block, block), lambda i, j: (i, j))
        spec_t = pl.BlockSpec((block, block), lambda i, j: (j, i))
        out_spec = pl.BlockSpec((None, block, block), lambda i, j: (j // per_part, i, j % per_part))
        return pl.pallas_call(_sym_only_kernel, grid=(count, count), in_specs=[spec, spec_t],
                              out_specs=out_spec, out_shape=out_shape)(half, half)
    spec = pl.BlockSpec((block, block), lambda i, j, f: (i, j))
    spec_t = pl.BlockSpec((block, block), lambda i, j, f: (j, i))
    out_spec = pl.BlockSpec((None, block, block), lambda i, j, f: (j // per_part, i, j % per_part))
    return pl.pallas_call(
        _sym_kernel,
        grid_spec=pltpu.PrefetchScalarGridSpec(
            num_scalar_prefetch=1, grid=(count, count),
            in_specs=[spec, spec_t, spec], out_specs=out_spec),
        out_shape=out_shape,
    )(jnp.reshape(flag.astype(jnp.int32), (1,)), half, half, other)


def row_bcast(value, source, targets):
    row = lax.axis_index("row")
    recv = None
    for target in targets:
        got = lax.ppermute(value, "row", [(source, target)])
        recv = got if recv is None else recv + got
    if recv is None:
        return value
    return jnp.where(row == source, value, recv)


def col_reduce_scatter(value, order):
    count = lax.axis_size("col")
    pos = lax.axis_index("col")
    bits = count.bit_length() - 1
    slab = value.shape[0] // count
    buf = value.reshape((2,) * bits + (slab,) + value.shape[1:])
    axes = [bits - 1 - b for b in range(bits)]
    for bit in order:
        axis = axes.index(bit)
        mine = (pos >> bit) % 2
        keep = lax.dynamic_index_in_dim(buf, mine, axis=axis, keepdims=False)
        send = lax.dynamic_index_in_dim(buf, 1 - mine, axis=axis, keepdims=False)
        buf = keep + lax.ppermute(send, "col", [(j, j ^ (1 << bit)) for j in range(count)])
        axes.pop(axis)
    return buf


def split_reduce_scatter(panels):
    bits = lax.axis_size("col").bit_length() - 1
    first = list(range(bits))
    second = [0] + list(range(bits - 1, 0, -1))
    return jnp.concatenate(
        [col_reduce_scatter(panels[0], first), col_reduce_scatter(panels[1], second)], axis=1)


def local(factor_rows, adjoint_rows, panel_inverse):
    row_count = lax.axis_size("row")
    panels = panel_inverse.shape[0]
    width = panel_inverse.shape[1]
    slab = factor_rows.shape[1]
    assert panels == 2 and factor_rows.shape[2] == width
    row = lax.axis_index("row")
    offset = lax.axis_index("col") * slab
    own1 = row_count - 1
    own0 = row_count - 2

    grow = offset + jnp.arange(slab, dtype=jnp.int32)[:, None]
    gcol = jnp.arange(width, dtype=jnp.int32)[None, :]
    lower = gcol <= grow
    diag_scale = jnp.where(gcol == grow, 0.5, 1.0).astype(jnp.float32)

    f0, f1 = factor_rows[0], factor_rows[1]
    a0, a1 = adjoint_rows[0], adjoint_rows[1]
    inv0, inv1 = panel_inverse[0], panel_inverse[1]

    full1 = lax.all_gather(f1, "col", axis=0, tiled=True)
    half1 = sandwich_half(phi(tmm(f1, jnp.where(lower, a1, 0.0))), inv1, split=False)
    part1 = sym_select(None, half1, None, parts=2)
    full1, part1 = lax.optimization_barrier((full1, part1))
    v1 = split_reduce_scatter(part1)
    diag1 = jnp.where(lower, v1, 0.0) * diag_scale
    f0_in, v1 = lax.optimization_barrier((f0, v1))
    full0 = lax.all_gather(f0_in, "col", axis=0, tiled=True)
    v1_near = jnp.where(row == own1, v1, lax.ppermute(v1, "row", [(own1, own0)]))
    a1_left = a1 - mm(v1_near, full1)

    col_adj = mm(a1_left, inv0)
    forward = jnp.stack([v1_near, col_adj])
    received = [lax.ppermute(forward, "row", [(own0, target)]) for target in range(own0)]
    x0 = tmm(f0, jnp.where(lower, a0, 0.0)) - lower_tmm(full0, jnp.tril(tmm(col_adj, f1)))
    part0 = sandwich_half(phi(x0), inv0)
    received, part0 = lax.optimization_barrier((received, part0))
    sent = sum(received[1:], received[0]) if received else forward
    cross = tmm(sent[1], f1, FAST)
    summed = split_reduce_scatter(sym_select(row == own0, part0, cross, parts=2))
    diag0 = jnp.where(lower, summed, 0.0) * diag_scale
    v0 = row_bcast(summed, own0, list(range(own0)))

    left1 = a1 - mm(sent[0], full1) - mm(sent[1], full0)
    left0 = a0 - summed - mm(v0, full0, FAST)
    out1 = jnp.where(row < own0, left1, jnp.where(row == own0, col_adj, diag1))
    out0 = jnp.where(row < own0, left0, jnp.where(row == own0, diag0, a0))
    return jnp.stack([out0, out1])


def solution(mesh):
    return jax.shard_map(
        local,
        mesh=mesh,
        in_specs=(P(None, "col", "row"), P(None, "col", "row"), P()),
        out_specs=P(None, "col", "row"),
        check_vma=False,
    )
```
